512 devices in a mesh: seq: 16 (over z, core), expert: 32 (over x, y).
Axes of the slice: x: 4, y: 8, z: 8, core: 2. Of those that a mesh axis runs over, the one named last changes fastest.
Arguments:
- hidden: bfloat16 [32, 1024, 2048], P('expert', 'seq'), may hold values from -6 to 6
- queries: bfloat16 [32, 1024, 4608], P('expert', 'seq'), may hold values from -5 to 5
- suffix_latent: bfloat16 [32, 1024, 576], P('expert', 'seq'), may hold values from -6 to 6
- prefix_latent: bfloat16 [2, 1024, 576], P(None, 'seq'), may hold values from -6 to 6
- lengths: int32 [32, 4], P('expert'), may hold values from 1 to 512, 1024 in all within a row
- prefix_of: int32 [32, 4], P('expert'), may hold values from 0 to 1
- value_up: bfloat16 [8, 512, 128], replicated, may hold values from -1 to 1
- out_proj: bfloat16 [1024, 2048], P(None, 'expert'), may hold values from -0.1875 to 0.1875
- norm_gain: float32 [2048], replicated, may hold values from 0.5 to 1.5
- router: bfloat16 [2048, 32], replicated, may hold values from -0.0625 to 0.0625
- routes: int32 [32, 1024, 6], P('expert', 'seq'), may hold values from 0 to 31, all different within a row; in each aligned block of 64 rows (0 to 63, 64 to 127, ..., all dimensions but the last counted through in order) at most 16 rows name the same one
- expert_in: bfloat16 [32, 2048, 1408], P('expert', 'seq'), may hold values from -0.125 to 0.125
- expert_out: bfloat16 [32, 2048, 704], P('expert', 'seq'), may hold values from -1.25 to 1.25
Outputs:
- layer_out: bfloat16 [32, 1024, 2048], P('expert', 'seq')
The draws below stay inside these ranges and needn't reach their ends.
Inputs may be any that keep to these rules, and one draw needn't show every extreme that they name: `routes`: among the rows of one device (aligned blocks of 64 tokens) no expert is named more than 16 times, a bound that some block reaches; a token's 6 experts differ. `lengths`: each row sums to 1024; its longest request has exactly 512 tokens.
All inputs are finite; a program needn't handle non-finite values.
Results may differ from the reference program's by a relative error of at most 0.013.
Values may be sent and summed in bfloat16 or wider, within the bound.
No kernel may reach another device: no remote copies, remote signals or barrier semaphores. Data moves between devices by JAX's collectives and lax.ppermute only.
A program may use at most 128 MiB of HBM per device.

```python
import functools
import math
import jax
import jax.numpy as jnp
import numpy as np
from jax import lax

D = 2048
HEADS = 8
LATENT = 512
ROPE = 64
VDIM = 128
HID = 704
TOP = 6
REQS = 4
TOK_DEV = 64
GROUPS = 32
EXPERTS = 32
SUF = 1024
PLEN = 1024
CAP = 16
N_SEQ = 16


def drawn_parts(key):
    base_key = jax.random.fold_in(key, 4711)
    sign_key, size_key, order_key, spot_key, row_key = jax.random.split(base_key, 5)
    key_width = LATENT + ROPE
    sign_pattern = jax.random.rademacher(sign_key, (key_width,), dtype=jnp.float32)
    magnitudes = 1.0 + jax.random.uniform(size_key, (2, key_width), jnp.float32)
    latent_order = jax.random.permutation(order_key, LATENT)
    prefix_spots = jax.random.randint(spot_key, (2,), 0, PLEN - 1)
    row_band = SUF // 3
    planted_rows = jax.random.randint(row_key, (GROUPS, 3), 0, row_band) + row_band * jnp.arange(3, dtype=jnp.int32)[None, :]
    return (sign_pattern, magnitudes, latent_order, prefix_spots, planted_rows)


def draw_prefix_latent(key, part):
    sign_pattern, magnitudes, latent_order, prefix_spots, planted_rows = drawn_parts(key)
    key_width = LATENT + ROPE
    noise_key = jax.random.fold_in(key, 11)
    noise_field = jnp.clip(jax.random.normal(noise_key, (2, PLEN, key_width), jnp.float32), -6.0, 6.0)
    rope_drop = 0.016 * key_width / ROPE
    top_key = sign_pattern[None, :] * magnitudes
    next_latent = sign_pattern[None, :LATENT] * magnitudes[:, :LATENT][:, latent_order]
    next_rope = sign_pattern[None, LATENT:] * (magnitudes[:, LATENT:] - rope_drop)
    next_key = jnp.concatenate([next_latent, next_rope], axis=1)
    positions = jnp.arange(PLEN, dtype=jnp.int32)
    hit_top = positions[None, :] == prefix_spots[:, None]
    hit_next = positions[None, :] == prefix_spots[:, None] + 1
    field = jnp.where(hit_top[:, :, None], top_key[:, None, :], noise_field)
    field = jnp.where(hit_next[:, :, None], next_key[:, None, :], field)
    return field.astype(jnp.bfloat16)


def draw_queries(key, part):
    sign_pattern, magnitudes, latent_order, prefix_spots, planted_rows = drawn_parts(key)
    key_width = LATENT + ROPE
    noise_key = jax.random.fold_in(key, 13)
    noise_field = jnp.clip(0.5 * jax.random.normal(noise_key, (GROUPS, SUF, HEADS * key_width), jnp.float32), -3.0, 3.0)
    strengths = jnp.array([1000.0, 1600.0, 2400.0], jnp.float32) / key_width
    positions = jnp.arange(SUF, dtype=jnp.int32)
    row_hit = positions[None, :, None] == planted_rows[:, None, :]
    strength = jnp.sum(jnp.where(row_hit, strengths[None, None, :], 0.0), axis=2)
    has_plant = jnp.any(row_hit, axis=2)
    pattern = jnp.tile(sign_pattern, HEADS)
    return jnp.where(has_plant[:, :, None], strength[:, :, None] * pattern[None, None, :], noise_field).astype(jnp.bfloat16)


def touch_ends(entries, key, smallest, top_value):
    place = [jax.random.randint(jax.random.fold_in(key, axis), (), 0, length) for axis, length in enumerate(entries.shape)]
    longest = entries.shape.index(max(entries.shape))
    neighbour = place[:longest] + [(place[longest] + 1) % entries.shape[longest]] + place[longest + 1:]
    return entries.at[tuple(place)].set(smallest).at[tuple(neighbour)].set(top_value)


def block_scale(rng, dims, shards, low, top_value):
    def one(position, shards_of):
        steps = jax.random.uniform(jax.random.fold_in(jax.random.fold_in(rng, 6), position), (shards_of,), jnp.float32, low / len(shards), top_value / len(shards))
        return jnp.repeat(jnp.exp(steps), dims[position] // shards_of).reshape((-1,) + (1,) * (len(dims) - position - 1))

    gain = one(*shards[0])
    for cut in shards[1:]:
        gain = gain * one(*cut)
    return gain


def length_profile(number_of, total, limit, slope):
    loads = [(1 << 20) // math.isqrt(grade ** slope) + 1 for grade in range(2, number_of + 1)]
    rest, given = total - limit - (number_of - 1), [1] * (number_of - 1)
    while rest > 0:
        candidates = [i for i in range(number_of - 1) if given[i] < limit]
        mass, budget = sum([loads[i] for i in candidates]), rest
        for i in candidates:
            more = min(limit - given[i], max(1, budget * loads[i] // mass), rest)
            given[i] = given[i] + more
            rest = rest - more
    return np.array([limit] + given)


def uneven(stream_key, amount, total, limit, skew):
    if amount == 2:
        one = jax.random.randint(stream_key, (), max(1, total - limit), min(limit, total - 1) + 1)
        return jnp.stack([one, total - one])
    sizes = jnp.asarray(length_profile(amount, total, limit, skew), jnp.int32)
    twos = (amount - 1) // 2
    giver, sink = sizes[1:1 + 2 * twos:2], sizes[2:2 + 2 * twos:2]
    room = jnp.minimum(giver - 1, limit - sink)
    shifted = jax.random.randint(jax.random.fold_in(stream_key, 1), (twos,), 0, 1 << 20) % (room + 1)
    sizes = sizes.at[1:1 + 2 * twos:2].set(giver - shifted).at[2:2 + 2 * twos:2].set(sink + shifted)
    return sizes[jax.random.permutation(jax.random.fold_in(stream_key, 2), amount)]


def shared_out(own_key, own, number, rows, number_of, top, bound, lean):
    order = jax.random.permutation(own_key, number_of)
    heavy_load, usual = portions_of(number_of, rows * top, bound, lean, True), portions_of(number_of, rows * top, bound, lean, False)
    places = jnp.arange(number_of)

    def named(tallies, turn):
        used = int((tallies > 0).sum())
        fixed = max(1, used // 4)
        passed = fixed + (places - fixed + turn * (used - fixed)) % max(1, number_of - fixed)
        return jnp.zeros((number_of,), jnp.int32).at[order[jnp.where(places < fixed, places, passed)]].set(jnp.asarray(tallies, jnp.int32))

    tallies = jnp.where(number % 4 == 0, named(heavy_load, number // 4), named(usual, number - number // 4 - 1))
    mixed = jax.random.permutation(jax.random.fold_in(own, 3), number_of)
    donor, receiver = mixed[0:number_of // 2 * 2:2], mixed[1:number_of // 2 * 2:2]
    margin = jnp.minimum(tallies[donor] - 1, bound - tallies[receiver]) // 2
    margin = jnp.where((donor == order[0]) | (receiver == order[0]) | (tallies[receiver] == 0), 0, jnp.maximum(margin, 0))
    passed = jax.random.randint(jax.random.fold_in(own, 4), (number_of // 2,), 0, 1 << 20) % (margin + 1)
    tallies = tallies.at[donor].add(-passed).at[receiver].add(passed)
    members = jnp.searchsorted(jnp.cumsum(tallies), jnp.arange(rows * top), side="right").astype(jnp.int32)
    table = members.reshape(top, rows).T
    table = table[jax.random.permutation(jax.random.fold_in(own, 1), rows)]
    turn = jax.random.randint(jax.random.fold_in(own, 2), (rows, 1), 0, top)
    return jnp.take_along_axis(table, (jnp.arange(top)[None, :] + turn) % top, axis=1)


def portions_of(count, total, reach, skew, full):
    loads = [(1 << 20) // math.isqrt(standing ** skew) + 1 for standing in range(1, count + 1)]
    largest = reach if full else min(reach, max(-(-total // count), total * loads[0] // sum(loads)))
    least = 1 if total - largest >= count - 1 else 0
    given, spare = [largest] + [least] * (count - 1), total - largest - least * (count - 1)
    while spare > 0:
        free = [i for i in range(1, count) if given[i] < largest] or [i for i in range(1, count) if given[i] < reach]
        whole, remaining = sum([loads[i] for i in free]), spare
        for i in free:
            addition = min(reach - given[i], max(1, remaining * loads[i] // whole), spare)
            given[i] = given[i] + addition
            spare = spare - addition
    return np.array(given)


def gaussian(rng, dims, spread, bound, cuts=(), kind=jnp.bfloat16):
    result = jax.random.normal(rng, dims, jnp.float32) * spread
    if len(cuts) > 0:
        result = block_scale(rng, dims, cuts, -0.22, 0.18) * result
    return jnp.clip(result, min=-bound, max=bound).astype(kind)


def setup_inputs(seed: int = 0) -> dict:
    keys = jax.random.split(jax.random.key(seed), 14)
    hidden = gaussian(keys[0], (GROUPS, SUF, D), 1.0, 6.0, ((0, 32), (1, 16)))
    queries = draw_queries(jax.random.fold_in(keys[13], 71), 0)
    suffix_latent = gaussian(keys[2], (GROUPS, SUF, LATENT + ROPE), 1.0, 6.0, ((0, 32), (1, 16)))
    prefix_latent = draw_prefix_latent(jax.random.fold_in(keys[13], 71), 0)
    lengths = jax.vmap(lambda own: uneven(own, REQS, SUF, SUF // 2, 2))(jax.random.split(keys[4], GROUPS)).reshape((GROUPS, REQS)).astype(jnp.int32)
    prefix_of = touch_ends(jax.random.randint(keys[5], (GROUPS, REQS), 0, 2), jax.random.fold_in(keys[5], 1), 0, 1).astype(jnp.int32)
    value_up = gaussian(keys[6], (HEADS, LATENT, VDIM), (LATENT // 16) ** -0.5, 1.0)
    out_proj = gaussian(keys[7], (HEADS * VDIM, D), (HEADS * VDIM) ** -0.5, 0.1875, ((1, 32),))
    norm_gain = jnp.clip(1.0 + 0.1 * jax.random.normal(keys[8], (D,), jnp.float32), 0.5, 1.5)
    router = gaussian(keys[9], (D, EXPERTS), (4 * D) ** -0.5, 0.0625)
    routes_keys = jax.random.split(jax.random.fold_in(keys[10], 1), GROUPS * SUF // TOK_DEV)
    routes_turns = jax.random.permutation(jax.random.fold_in(keys[10], 3), GROUPS * SUF // TOK_DEV)
    routes = jax.vmap(lambda own, number: shared_out(jax.random.fold_in(keys[10], 2), own, number, TOK_DEV, EXPERTS, TOP, CAP, 2))(routes_keys, routes_turns).reshape((GROUPS, SUF, TOP))
    expert_in = gaussian(keys[11], (EXPERTS, D, 2 * HID), D ** -0.5, 0.125, ((0, 32), (1, 16)))
    expert_out = gaussian(keys[12], (EXPERTS, D, HID), (max(1, HID // 36)) ** -0.5, 1.25, ((0, 32), (1, 16)))
    return dict(hidden=hidden, queries=queries, suffix_latent=suffix_latent, prefix_latent=prefix_latent, lengths=lengths, prefix_of=prefix_of, value_up=value_up, out_proj=out_proj, norm_gain=norm_gain, router=router, routes=routes, expert_in=expert_in, expert_out=expert_out)


qk_scale = 192.0 ** (-0.5)
big_negative = -1e+30
highest = lax.Precision.HIGHEST

def request_of(positions, request_ends):
    return lax.optimization_barrier(jnp.sum((positions[:, None] >= request_ends[None, :]).astype(jnp.int32), axis=1))

def attend_group(operands, prefix_latent):
    group_queries, group_suffix, group_lengths, group_choice = operands
    total_tokens = group_suffix.shape[0]
    key_width = group_suffix.shape[1]
    head_count = group_queries.shape[1] // key_width
    latent_width = key_width - ROPE
    query_rows = group_queries.astype(jnp.float32).reshape(total_tokens, head_count, key_width)
    request_ends = jnp.cumsum(group_lengths)
    positions = jnp.arange(total_tokens, dtype=jnp.int32)
    requests = request_of(positions, request_ends)
    request_ids = jnp.arange(group_lengths.shape[0], dtype=jnp.int32)
    chosen = lax.optimization_barrier(jnp.sum(jnp.where(requests[:, None] == request_ids[None, :], group_choice[None, :], 0), axis=1))
    suffix_keys = group_suffix.astype(jnp.float32)
    prefix_keys = prefix_latent.astype(jnp.float32)
    suffix_scores = jnp.einsum('thk,sk->ths', query_rows, suffix_keys, precision=highest) * qk_scale
    prefix_scores = jnp.einsum('thk,pnk->thpn', query_rows, prefix_keys, precision=highest) * qk_scale
    prefix_scores = prefix_scores.reshape(total_tokens, head_count, 2 * PLEN)
    suffix_allowed = (requests[:, None] == requests[None, :]) & (positions[None, :] <= positions[:, None])
    prefix_pick = chosen[:, None] == jnp.arange(2, dtype=jnp.int32)[None, :]
    prefix_allowed = jnp.broadcast_to(prefix_pick[:, :, None], (total_tokens, 2, PLEN)).reshape(total_tokens, 2 * PLEN)
    allowed = jnp.concatenate([suffix_allowed, prefix_allowed], axis=1)[:, None, :]
    scores = jnp.concatenate([suffix_scores, prefix_scores], axis=2)
    top_score = lax.optimization_barrier(jnp.max(jnp.where(allowed, scores, big_negative), axis=2, keepdims=True))
    weights = jnp.where(allowed, jnp.exp(scores - top_score), 0.0)
    denominator = lax.optimization_barrier(jnp.sum(weights, axis=2))
    rounded_weights = lax.optimization_barrier(weights.astype(jnp.bfloat16)).astype(jnp.float32)
    values = jnp.concatenate([suffix_keys[:, :latent_width], prefix_keys[:, :, :latent_width].reshape(2 * PLEN, latent_width)], axis=0)
    summed = jnp.einsum('ths,sl->thl', rounded_weights, values, precision=highest)
    return (summed / denominator[:, :, None]).astype(jnp.bfloat16)

def reference(hidden, queries, suffix_latent, prefix_latent, lengths, prefix_of, value_up, out_proj, norm_gain, router, routes, expert_in, expert_out):
    attend = functools.partial(attend_group, prefix_latent=prefix_latent)
    latent_out = lax.map(attend, (queries, suffix_latent, lengths, prefix_of))
    value_out = jnp.einsum('gthl,hlv->gthv', latent_out.astype(jnp.float32), value_up.astype(jnp.float32)).astype(jnp.bfloat16)
    value_out = value_out.reshape(GROUPS * SUF, HEADS * VDIM)
    residual = hidden.astype(jnp.float32).reshape(GROUPS * SUF, D) + jnp.dot(value_out, out_proj, preferred_element_type=jnp.float32)
    normed = (residual * lax.rsqrt(lax.optimization_barrier(jnp.mean(residual * residual, axis=1, keepdims=True)) + 1e-06) * norm_gain).astype(jnp.bfloat16)
    logits = jnp.dot(normed, router, preferred_element_type=jnp.float32)
    expert_probs = jax.nn.softmax(logits, axis=1)
    block_count = GROUPS * N_SEQ
    route_blocks = routes.reshape(block_count, TOK_DEV, TOP)
    expert_ids = jnp.arange(EXPERTS, dtype=jnp.int32)
    matches = route_blocks[:, :, :, None] == expert_ids[None, None, None, :]
    gate_values = lax.optimization_barrier(jnp.sum(jnp.where(matches, expert_probs.reshape(block_count, TOK_DEV, 1, EXPERTS), 0.0), axis=3))
    flat_hits = matches.reshape(block_count, TOK_DEV * TOP, EXPERTS).astype(jnp.int32)
    earlier = jnp.cumsum(flat_hits, axis=1) - flat_hits
    slot_index = lax.optimization_barrier(jnp.sum(earlier * flat_hits, axis=2)).reshape(block_count, TOK_DEV, TOP)
    normed_blocks = normed.reshape(block_count, TOK_DEV, D)
    block_ids = jnp.broadcast_to(jnp.arange(block_count, dtype=jnp.int32)[:, None], (block_count, TOK_DEV))

    def expert_step(combined, operands):
        expert_id, weight_in, weight_out = operands
        hits = route_blocks == expert_id
        has_hit = jnp.any(hits, axis=2)
        slot = lax.optimization_barrier(jnp.sum(jnp.where(hits, slot_index, 0), axis=2)).astype(jnp.int32)
        gate = lax.optimization_barrier(jnp.sum(jnp.where(hits, gate_values, 0.0), axis=2))
        target = jnp.where(has_hit, slot, CAP).astype(jnp.int32)
        buffer = jnp.zeros((block_count, CAP, D), jnp.bfloat16).at[block_ids, target].set(normed_blocks, mode='drop')
        gate_up = jnp.dot(buffer.reshape(block_count * CAP, D), weight_in, preferred_element_type=jnp.float32)
        active = (jax.nn.silu(gate_up[:, :HID]) * gate_up[:, HID:]).astype(jnp.bfloat16)
        produced = jnp.dot(active, weight_out.T, preferred_element_type=jnp.float32).astype(jnp.bfloat16)
        produced = produced.reshape(block_count, CAP, D)
        picked = produced[block_ids, jnp.minimum(slot, CAP - 1).astype(jnp.int32)]
        return (combined + gate[:, :, None] * picked.astype(jnp.float32), None)
    start_sum = jnp.zeros((block_count, TOK_DEV, D), jnp.float32)
    combined, unused = lax.scan(expert_step, start_sum, (expert_ids, expert_in, expert_out))
    layer_out = residual + combined.reshape(GROUPS * SUF, D)
    return layer_out.astype(jnp.bfloat16).reshape(GROUPS, SUF, D)
```

```python
import jax
import jax.numpy as jnp
from jax import lax
from jax.sharding import PartitionSpec as P

qk_scale = 192.0 ** (-0.5)
big_negative = -1e30


def request_of(positions, request_ends):
    return jnp.sum((positions[:, None] >= request_ends[None, :]).astype(jnp.int32), axis=1)


def merge_scores(running, scores, allowed, values):
    running_max, running_sum, running_acc = running
    new_max = jnp.maximum(running_max, jnp.max(jnp.where(allowed, scores, big_negative), axis=2))
    weights = jnp.where(allowed, jnp.exp(scores - new_max[:, :, None]), 0.0)
    new_sum = jnp.sum(weights, axis=2)
    new_acc = jnp.einsum(
        "thn,nl->thl", weights.astype(jnp.bfloat16), values, preferred_element_type=jnp.float32
    )
    return (new_max, new_sum, new_acc)


def local(
    hidden,
    queries,
    suffix_latent,
    prefix_latent,
    lengths,
    prefix_of,
    value_up,
    out_proj,
    norm_gain,
    router,
    routes,
    expert_in,
    expert_out,
):
    local_tokens = hidden.shape[1]
    model_width = hidden.shape[2]
    key_width = suffix_latent.shape[2]
    head_count = value_up.shape[0]
    latent_width = value_up.shape[1]
    expert_count = router.shape[1]
    top_count = routes.shape[2]
    capacity = 4 * local_tokens * top_count // (3 * expert_count)
    request_count = lengths.shape[1]
    request_ends = jnp.cumsum(lengths[0])
    my_positions = lax.axis_index("seq") * local_tokens + jnp.arange(local_tokens, dtype=jnp.int32)
    my_requests = request_of(my_positions, request_ends)
    request_ids = jnp.arange(request_count, dtype=jnp.int32)
    chosen = jnp.sum(
        jnp.where(my_requests[:, None] == request_ids[None, :], prefix_of[0][None, :], 0), axis=1
    )
    prefix_pick = chosen[:, None] == jnp.arange(2, dtype=jnp.int32)[None, :]
    single_prefix = jnp.all(chosen == chosen[0])
    my_prefix = chosen[0]
    query_rows = queries[0].reshape(local_tokens, head_count, key_width)
    start_state = (
        jnp.full((local_tokens, head_count), big_negative, jnp.float32),
        jnp.zeros((local_tokens, head_count), jnp.float32),
        jnp.zeros((local_tokens, head_count, latent_width), jnp.float32),
    )
    key_stack = jnp.concatenate([suffix_latent, prefix_latent], axis=0)
    key_stack = lax.all_gather(key_stack, "seq", axis=1, tiled=True)
    suffix_piece = key_stack[:1]
    prefix_piece = key_stack[1:]
    piece_rows = suffix_piece.shape[1]
    suffix_keys = suffix_piece[0]
    key_positions = jnp.arange(piece_rows, dtype=jnp.int32)
    key_requests = request_of(key_positions, request_ends)
    suffix_allowed = (key_requests[None, :] == my_requests[:, None]) & (
        key_positions[None, :] <= my_positions[:, None]
    )
    suffix_scores = (
        jnp.einsum("thk,nk->thn", query_rows, suffix_keys, preferred_element_type=jnp.float32)
        * qk_scale
    )

    def one_prefix(running_state):
        chosen_keys = lax.dynamic_index_in_dim(prefix_piece, my_prefix, 0, keepdims=False)
        prefix_scores = (
            jnp.einsum("thk,nk->thn", query_rows, chosen_keys, preferred_element_type=jnp.float32)
            * qk_scale
        )
        scores = jnp.concatenate([suffix_scores, prefix_scores], axis=2)
        every_key = jnp.ones((local_tokens, piece_rows), dtype=bool)
        allowed = jnp.concatenate([suffix_allowed, every_key], axis=1)[:, None, :]
        values = jnp.concatenate(
            [suffix_keys[:, :latent_width], chosen_keys[:, :latent_width]], axis=0
        )
        return merge_scores(running_state, scores, allowed, values)

    def two_prefixes(running_state):
        prefix_scores = (
            jnp.einsum(
                "thk,pnk->thpn", query_rows, prefix_piece, preferred_element_type=jnp.float32
            )
            * qk_scale
        )
        scores = jnp.concatenate(
            [suffix_scores, prefix_scores.reshape(local_tokens, head_count, 2 * piece_rows)], axis=2
        )
        prefix_allowed = jnp.broadcast_to(
            prefix_pick[:, :, None], (local_tokens, 2, piece_rows)
        ).reshape(local_tokens, 2 * piece_rows)
        allowed = jnp.concatenate([suffix_allowed, prefix_allowed], axis=1)[:, None, :]
        values = jnp.concatenate(
            [
                suffix_keys[:, :latent_width],
                prefix_piece[:, :, :latent_width].reshape(2 * piece_rows, latent_width),
            ],
            axis=0,
        )
        return merge_scores(running_state, scores, allowed, values)

    final_max, final_sum, final_acc = lax.cond(single_prefix, one_prefix, two_prefixes, start_state)
    latent_out = (final_acc / final_sum[:, :, None]).astype(jnp.bfloat16)
    value_out = jnp.einsum(
        "thl,hlv->thv", latent_out, value_up, preferred_element_type=jnp.float32
    ).astype(jnp.bfloat16)
    value_out = value_out.reshape(local_tokens, head_count * value_up.shape[2])
    expert_devices = model_width // out_proj.shape[1]
    column_blocks = lax.all_to_all(
        jnp.broadcast_to(out_proj[None], (expert_devices,) + out_proj.shape),
        "expert",
        split_axis=0,
        concat_axis=0,
        tiled=True,
    )
    projected = jnp.einsum(
        "tr,jrc->tjc", value_out, column_blocks, preferred_element_type=jnp.float32
    ).reshape(local_tokens, model_width)
    residual = hidden[0].astype(jnp.float32) + projected
    normed = (
        residual
        * lax.rsqrt(jnp.mean(residual * residual, axis=1, keepdims=True) + 1e-06)
        * norm_gain
    ).astype(jnp.bfloat16)
    logits = jnp.dot(normed, router, preferred_element_type=jnp.float32)
    expert_probs = jax.nn.softmax(logits, axis=1)
    expert_ids = jnp.arange(expert_count, dtype=jnp.int32)
    my_routes = routes[0]
    matches = my_routes[:, :, None] == expert_ids[None, None, :]
    gate_values = jnp.sum(jnp.where(matches, expert_probs[:, None, :], 0.0), axis=2)
    flat_hits = matches.reshape(local_tokens * top_count, expert_count).astype(jnp.int32)
    earlier = jnp.cumsum(flat_hits, axis=0) - flat_hits
    slot_index = jnp.sum(earlier * flat_hits, axis=1).reshape(local_tokens, top_count)
    cell_index = my_routes * capacity + slot_index
    cell_ids = jnp.arange(expert_count * capacity, dtype=jnp.int32)
    placing = jnp.sum(
        (cell_ids[:, None, None] == cell_index[None, :, :]).astype(jnp.int32), axis=2
    ).astype(jnp.bfloat16)
    outgoing = jnp.dot(placing, normed, preferred_element_type=jnp.float32).astype(jnp.bfloat16)
    outgoing = outgoing.reshape(expert_count, capacity, model_width)
    incoming = lax.all_to_all(outgoing, "expert", split_axis=0, concat_axis=0, tiled=True)
    in_width = expert_in.shape[2]
    full_both = lax.all_gather(
        jnp.concatenate([expert_in, expert_out], axis=2), "seq", axis=1, tiled=True
    )
    full_in, full_out = full_both[:, :, :in_width], full_both[:, :, in_width:]
    all_rows = incoming.reshape(-1, model_width)
    gate_up = jnp.dot(all_rows, full_in[0], preferred_element_type=jnp.float32)
    hidden_units = gate_up.shape[1] // 2
    active = (jax.nn.silu(gate_up[:, :hidden_units]) * gate_up[:, hidden_units:]).astype(
        jnp.bfloat16
    )
    produced = lax.dot_general(
        active, full_out[0], (((1,), (1,)), ((), ())), preferred_element_type=jnp.float32
    ).astype(jnp.bfloat16)
    returned = lax.all_to_all(
        produced.reshape(-1, capacity, model_width),
        "expert",
        split_axis=0,
        concat_axis=0,
        tiled=True,
    )
    returned_rows = returned.reshape(-1, model_width)
    picked = returned_rows[cell_index]
    routed_sum = jnp.sum(gate_values[:, :, None] * picked.astype(jnp.float32), axis=1)
    layer_out = (residual + routed_sum).astype(jnp.bfloat16)
    return layer_out[None]


def solution(mesh):
    in_specs = (
        P("expert", "seq", None),
        P("expert", "seq", None),
        P("expert", "seq", None),
        P(None, "seq", None),
        P("expert", None),
        P("expert", None),
        P(),
        P(None, "expert"),
        P(),
        P(),
        P("expert", "seq", None),
        P("expert", "seq", None),
        P("expert", "seq", None),
    )
    out_specs = P("expert", "seq", None)
    return jax.shard_map(local, mesh=mesh, in_specs=in_specs, out_specs=out_specs, check_vma=False)
```

```python
import functools

import jax
import jax.numpy as jnp
from jax import lax
from jax.sharding import PartitionSpec as P

qk_scale = 192.0 ** (-0.5)
big_negative = -1e30


def request_of(positions, request_ends):
    return jnp.sum((positions[:, None] >= request_ends[None, :]).astype(jnp.int32), axis=1)


def merge_scores(running, scores, allowed, values):
    running_max, running_sum, running_acc = running
    new_max = jnp.maximum(running_max, jnp.max(jnp.where(allowed, scores, big_negative), axis=2))
    weights = jnp.where(allowed, jnp.exp(scores - new_max[:, :, None]), 0.0)
    new_sum = jnp.sum(weights, axis=2)
    new_acc = jnp.einsum(
        "thn,nl->thl", weights.astype(jnp.bfloat16), values, preferred_element_type=jnp.float32
    )
    return (new_max, new_sum, new_acc)


def local(
    hidden,
    queries,
    suffix_latent,
    prefix_latent,
    lengths,
    prefix_of,
    value_up,
    out_proj,
    norm_gain,
    router,
    routes,
    expert_in,
    expert_out,
    seq_count=1,
):
    local_tokens = hidden.shape[1]
    model_width = hidden.shape[2]
    key_width = suffix_latent.shape[2]
    head_count = value_up.shape[0]
    latent_width = value_up.shape[1]
    expert_count = router.shape[1]
    top_count = routes.shape[2]
    capacity = 4 * local_tokens * top_count // (3 * expert_count)
    request_count = lengths.shape[1]
    request_ends = jnp.cumsum(lengths[0])
    my_positions = lax.axis_index("seq") * local_tokens + jnp.arange(local_tokens, dtype=jnp.int32)
    my_requests = request_of(my_positions, request_ends)
    request_ids = jnp.arange(request_count, dtype=jnp.int32)
    chosen = jnp.sum(
        jnp.where(my_requests[:, None] == request_ids[None, :], prefix_of[0][None, :], 0), axis=1
    )
    prefix_pick = chosen[:, None] == jnp.arange(2, dtype=jnp.int32)[None, :]
    single_prefix = jnp.all(chosen == chosen[0])
    my_prefix = chosen[0]
    query_rows = queries[0].reshape(local_tokens, head_count, key_width)
    start_state = (
        jnp.full((local_tokens, head_count), big_negative, jnp.float32),
        jnp.zeros((local_tokens, head_count), jnp.float32),
        jnp.zeros((local_tokens, head_count, latent_width), jnp.float32),
    )
    key_stack = jnp.concatenate([suffix_latent, prefix_latent], axis=0)
    key_stack = lax.all_gather(key_stack, "seq", axis=1, tiled=True)
    suffix_piece = key_stack[:1]
    prefix_piece = key_stack[1:]
    piece_rows = suffix_piece.shape[1]
    suffix_keys = suffix_piece[0]
    key_positions = jnp.arange(piece_rows, dtype=jnp.int32)
    key_requests = request_of(key_positions, request_ends)
    suffix_allowed = (key_requests[None, :] == my_requests[:, None]) & (
        key_positions[None, :] <= my_positions[:, None]
    )
    suffix_scores = (
        jnp.einsum("thk,nk->thn", query_rows, suffix_keys, preferred_element_type=jnp.float32)
        * qk_scale
    )

    def one_prefix(running_state):
        chosen_keys = lax.dynamic_index_in_dim(prefix_piece, my_prefix, 0, keepdims=False)
        prefix_scores = (
            jnp.einsum("thk,nk->thn", query_rows, chosen_keys, preferred_element_type=jnp.float32)
            * qk_scale
        )
        scores = jnp.concatenate([suffix_scores, prefix_scores], axis=2)
        every_key = jnp.ones((local_tokens, piece_rows), dtype=bool)
        allowed = jnp.concatenate([suffix_allowed, every_key], axis=1)[:, None, :]
        values = jnp.concatenate(
            [suffix_keys[:, :latent_width], chosen_keys[:, :latent_width]], axis=0
        )
        return merge_scores(running_state, scores, allowed, values)

    def two_prefixes(running_state):
        prefix_scores = (
            jnp.einsum(
                "thk,pnk->thpn", query_rows, prefix_piece, preferred_element_type=jnp.float32
            )
            * qk_scale
        )
        scores = jnp.concatenate(
            [suffix_scores, prefix_scores.reshape(local_tokens, head_count, 2 * piece_rows)], axis=2
        )
        prefix_allowed = jnp.broadcast_to(
            prefix_pick[:, :, None], (local_tokens, 2, piece_rows)
        ).reshape(local_tokens, 2 * piece_rows)
        allowed = jnp.concatenate([suffix_allowed, prefix_allowed], axis=1)[:, None, :]
        values = jnp.concatenate(
            [
                suffix_keys[:, :latent_width],
                prefix_piece[:, :, :latent_width].reshape(2 * piece_rows, latent_width),
            ],
            axis=0,
        )
        return merge_scores(running_state, scores, allowed, values)

    final_max, final_sum, final_acc = lax.cond(single_prefix, one_prefix, two_prefixes, start_state)
    latent_out = (final_acc / final_sum[:, :, None]).astype(jnp.bfloat16)
    value_out = jnp.einsum(
        "thl,hlv->thv", latent_out, value_up, preferred_element_type=jnp.float32
    ).astype(jnp.bfloat16)
    value_out = value_out.reshape(local_tokens, head_count * value_up.shape[2])
    expert_devices = model_width // out_proj.shape[1]
    half_rows = out_proj.shape[0] // 2
    core = lax.axis_index("seq") % 2
    my_rows = lax.dynamic_slice_in_dim(out_proj, core * half_rows, half_rows, axis=0)
    my_blocks = lax.all_to_all(
        jnp.broadcast_to(my_rows[None], (expert_devices,) + my_rows.shape),
        "expert",
        split_axis=0,
        concat_axis=0,
        tiled=True,
    )
    other_blocks = lax.ppermute(
        my_blocks, "seq", perm=[(i, i ^ 1) for i in range(seq_count)]
    )
    my_part = lax.dynamic_slice_in_dim(value_out, core * half_rows, half_rows, axis=1)
    other_part = lax.dynamic_slice_in_dim(value_out, (1 - core) * half_rows, half_rows, axis=1)
    projected = (
        jnp.einsum("tr,jrc->tjc", my_part, my_blocks, preferred_element_type=jnp.float32)
        + jnp.einsum("tr,jrc->tjc", other_part, other_blocks, preferred_element_type=jnp.float32)
    ).reshape(local_tokens, model_width)
    residual = hidden[0].astype(jnp.float32) + projected
    normed = (
        residual
        * lax.rsqrt(jnp.mean(residual * residual, axis=1, keepdims=True) + 1e-06)
        * norm_gain
    ).astype(jnp.bfloat16)
    logits = jnp.dot(normed, router, preferred_element_type=jnp.float32)
    expert_probs = jax.nn.softmax(logits, axis=1)
    expert_ids = jnp.arange(expert_count, dtype=jnp.int32)
    my_routes = routes[0]
    matches = my_routes[:, :, None] == expert_ids[None, None, :]
    gate_values = jnp.sum(jnp.where(matches, expert_probs[:, None, :], 0.0), axis=2)
    flat_hits = matches.reshape(local_tokens * top_count, expert_count).astype(jnp.int32)
    earlier = jnp.cumsum(flat_hits, axis=0) - flat_hits
    slot_index = jnp.sum(earlier * flat_hits, axis=1).reshape(local_tokens, top_count)
    cell_index = my_routes * capacity + slot_index
    cell_ids = jnp.arange(expert_count * capacity, dtype=jnp.int32)
    placing = jnp.sum(
        (cell_ids[:, None, None] == cell_index[None, :, :]).astype(jnp.int32), axis=2
    ).astype(jnp.bfloat16)
    outgoing = jnp.dot(placing, normed, preferred_element_type=jnp.float32).astype(jnp.bfloat16)
    outgoing = outgoing.reshape(expert_count, capacity, model_width)
    incoming = lax.all_to_all(outgoing, "expert", split_axis=0, concat_axis=0, tiled=True)
    in_width = expert_in.shape[2]
    full_both = lax.all_gather(
        jnp.concatenate([expert_in, expert_out], axis=2), "seq", axis=1, tiled=True
    )
    full_in, full_out = full_both[:, :, :in_width], full_both[:, :, in_width:]
    all_rows = incoming.reshape(-1, model_width)
    gate_up = jnp.dot(all_rows, full_in[0], preferred_element_type=jnp.float32)
    hidden_units = gate_up.shape[1] // 2
    active = (jax.nn.silu(gate_up[:, :hidden_units]) * gate_up[:, hidden_units:]).astype(
        jnp.bfloat16
    )
    produced = lax.dot_general(
        active, full_out[0], (((1,), (1,)), ((), ())), preferred_element_type=jnp.float32
    ).astype(jnp.bfloat16)
    returned = lax.all_to_all(
        produced.reshape(-1, capacity, model_width),
        "expert",
        split_axis=0,
        concat_axis=0,
        tiled=True,
    )
    returned_rows = returned.reshape(-1, model_width)
    picked = returned_rows[cell_index]
    routed_sum = jnp.sum(gate_values[:, :, None] * picked.astype(jnp.float32), axis=1)
    layer_out = (residual + routed_sum).astype(jnp.bfloat16)
    return layer_out[None]


def solution(mesh):
    in_specs = (
        P("expert", "seq", None),
        P("expert", "seq", None),
        P("expert", "seq", None),
        P(None, "seq", None),
        P("expert", None),
        P("expert", None),
        P(),
        P(None, "expert"),
        P(),
        P(),
        P("expert", "seq", None),
        P("expert", "seq", None),
        P("expert", "seq", None),
    )
    out_specs = P("expert", "seq", None)
    return jax.shard_map(functools.partial(local, seq_count=mesh.shape["seq"]), mesh=mesh, in_specs=in_specs, out_specs=out_specs, check_vma=False)
```

```python
import functools

import jax
import jax.numpy as jnp
from jax import lax
from jax.sharding import PartitionSpec as P

qk_scale = 192.0 ** (-0.5)
big_negative = -1e30


def request_of(positions, request_ends):
    return jnp.sum((positions[:, None] >= request_ends[None, :]).astype(jnp.int32), axis=1)


def merge_scores(running, scores, allowed, values):
    running_max, running_sum, running_acc = running
    new_max = jnp.maximum(running_max, jnp.max(jnp.where(allowed, scores, big_negative), axis=2))
    weights = jnp.where(allowed, jnp.exp(scores - new_max[:, :, None]), 0.0)
    new_sum = jnp.sum(weights, axis=2)
    new_acc = jnp.einsum(
        "thn,nl->thl", weights.astype(jnp.bfloat16), values, preferred_element_type=jnp.float32
    )
    return (new_max, new_sum, new_acc)


def local(
    hidden,
    queries,
    suffix_latent,
    prefix_latent,
    lengths,
    prefix_of,
    value_up,
    out_proj,
    norm_gain,
    router,
    routes,
    expert_in,
    expert_out,
    seq_count=1,
):
    local_tokens = hidden.shape[1]
    model_width = hidden.shape[2]
    key_width = suffix_latent.shape[2]
    head_count = value_up.shape[0]
    latent_width = value_up.shape[1]
    expert_count = router.shape[1]
    top_count = routes.shape[2]
    capacity = 4 * local_tokens * top_count // (3 * expert_count)
    request_count = lengths.shape[1]
    request_ends = jnp.cumsum(lengths[0])
    my_positions = lax.axis_index("seq") * local_tokens + jnp.arange(local_tokens, dtype=jnp.int32)
    my_requests = request_of(my_positions, request_ends)
    request_ids = jnp.arange(request_count, dtype=jnp.int32)
    chosen = jnp.sum(
        jnp.where(my_requests[:, None] == request_ids[None, :], prefix_of[0][None, :], 0), axis=1
    )
    prefix_pick = chosen[:, None] == jnp.arange(2, dtype=jnp.int32)[None, :]
    single_prefix = jnp.all(chosen == chosen[0])
    my_prefix = chosen[0]
    query_rows = queries[0].reshape(local_tokens, head_count, key_width)
    start_state = (
        jnp.full((local_tokens, head_count), big_negative, jnp.float32),
        jnp.zeros((local_tokens, head_count), jnp.float32),
        jnp.zeros((local_tokens, head_count, latent_width), jnp.float32),
    )
    key_stack = jnp.concatenate([suffix_latent, prefix_latent], axis=0)
    key_stack = lax.all_gather(key_stack, "seq", axis=1, tiled=True)
    suffix_piece = key_stack[:1]
    prefix_piece = key_stack[1:]
    piece_rows = suffix_piece.shape[1]
    suffix_keys = suffix_piece[0]
    key_positions = jnp.arange(piece_rows, dtype=jnp.int32)
    key_requests = request_of(key_positions, request_ends)
    suffix_allowed = (key_requests[None, :] == my_requests[:, None]) & (
        key_positions[None, :] <= my_positions[:, None]
    )
    suffix_scores = (
        jnp.einsum("thk,nk->thn", query_rows, suffix_keys, preferred_element_type=jnp.float32)
        * qk_scale
    )

    def one_prefix(running_state):
        chosen_keys = lax.dynamic_index_in_dim(prefix_piece, my_prefix, 0, keepdims=False)
        prefix_scores = (
            jnp.einsum("thk,nk->thn", query_rows, chosen_keys, preferred_element_type=jnp.float32)
            * qk_scale
        )
        scores = jnp.concatenate([suffix_scores, prefix_scores], axis=2)
        every_key = jnp.ones((local_tokens, piece_rows), dtype=bool)
        allowed = jnp.concatenate([suffix_allowed, every_key], axis=1)[:, None, :]
        values = jnp.concatenate(
            [suffix_keys[:, :latent_width], chosen_keys[:, :latent_width]], axis=0
        )
        return merge_scores(running_state, scores, allowed, values)

    def two_prefixes(running_state):
        prefix_scores = (
            jnp.einsum(
                "thk,pnk->thpn", query_rows, prefix_piece, preferred_element_type=jnp.float32
            )
            * qk_scale
        )
        scores = jnp.concatenate(
            [suffix_scores, prefix_scores.reshape(local_tokens, head_count, 2 * piece_rows)], axis=2
        )
        prefix_allowed = jnp.broadcast_to(
            prefix_pick[:, :, None], (local_tokens, 2, piece_rows)
        ).reshape(local_tokens, 2 * piece_rows)
        allowed = jnp.concatenate([suffix_allowed, prefix_allowed], axis=1)[:, None, :]
        values = jnp.concatenate(
            [
                suffix_keys[:, :latent_width],
                prefix_piece[:, :, :latent_width].reshape(2 * piece_rows, latent_width),
            ],
            axis=0,
        )
        return merge_scores(running_state, scores, allowed, values)

    final_max, final_sum, final_acc = lax.cond(single_prefix, one_prefix, two_prefixes, start_state)
    latent_out = (final_acc / final_sum[:, :, None]).astype(jnp.bfloat16)
    value_out = jnp.einsum(
        "thl,hlv->thv", latent_out, value_up, preferred_element_type=jnp.float32
    ).astype(jnp.bfloat16)
    value_out = value_out.reshape(local_tokens, head_count * value_up.shape[2])
    expert_devices = model_width // out_proj.shape[1]
    half_rows = out_proj.shape[0] // 2
    core = lax.axis_index("seq") % 2
    my_rows = lax.dynamic_slice_in_dim(out_proj, core * half_rows, half_rows, axis=0)
    my_blocks = lax.all_to_all(
        jnp.broadcast_to(my_rows[None], (expert_devices,) + my_rows.shape),
        "expert",
        split_axis=0,
        concat_axis=0,
        tiled=True,
    )
    my_blocks, value_out = lax.optimization_barrier((my_blocks, value_out))
    other_blocks = lax.ppermute(
        my_blocks, "seq", perm=[(i, i ^ 1) for i in range(seq_count)]
    )
    my_part = lax.dynamic_slice_in_dim(value_out, core * half_rows, half_rows, axis=1)
    other_part = lax.dynamic_slice_in_dim(value_out, (1 - core) * half_rows, half_rows, axis=1)
    projected = (
        jnp.einsum("tr,jrc->tjc", my_part, my_blocks, preferred_element_type=jnp.float32)
        + jnp.einsum("tr,jrc->tjc", other_part, other_blocks, preferred_element_type=jnp.float32)
    ).reshape(local_tokens, model_width)
    residual = hidden[0].astype(jnp.float32) + projected
    normed = (
        residual
        * lax.rsqrt(jnp.mean(residual * residual, axis=1, keepdims=True) + 1e-06)
        * norm_gain
    ).astype(jnp.bfloat16)
    logits = jnp.dot(normed, router, preferred_element_type=jnp.float32)
    expert_probs = jax.nn.softmax(logits, axis=1)
    expert_ids = jnp.arange(expert_count, dtype=jnp.int32)
    my_routes = routes[0]
    matches = my_routes[:, :, None] == expert_ids[None, None, :]
    gate_values = jnp.sum(jnp.where(matches, expert_probs[:, None, :], 0.0), axis=2)
    flat_hits = matches.reshape(local_tokens * top_count, expert_count).astype(jnp.int32)
    earlier = jnp.cumsum(flat_hits, axis=0) - flat_hits
    slot_index = jnp.sum(earlier * flat_hits, axis=1).reshape(local_tokens, top_count)
    cell_index = my_routes * capacity + slot_index
    cell_ids = jnp.arange(expert_count * capacity, dtype=jnp.int32)
    placing = jnp.sum(
        (cell_ids[:, None, None] == cell_index[None, :, :]).astype(jnp.int32), axis=2
    ).astype(jnp.bfloat16)
    outgoing = jnp.dot(placing, normed, preferred_element_type=jnp.float32).astype(jnp.bfloat16)
    outgoing = outgoing.reshape(expert_count, capacity, model_width)
    incoming = lax.all_to_all(outgoing, "expert", split_axis=0, concat_axis=0, tiled=True)
    in_width = expert_in.shape[2]
    full_both = lax.all_gather(
        jnp.concatenate([expert_in, expert_out], axis=2), "seq", axis=1, tiled=True
    )
    full_in, full_out = full_both[:, :, :in_width], full_both[:, :, in_width:]
    all_rows = incoming.reshape(-1, model_width)
    gate_up = jnp.dot(all_rows, full_in[0], preferred_element_type=jnp.float32)
    hidden_units = gate_up.shape[1] // 2
    active = (jax.nn.silu(gate_up[:, :hidden_units]) * gate_up[:, hidden_units:]).astype(
        jnp.bfloat16
    )
    produced = lax.dot_general(
        active, full_out[0], (((1,), (1,)), ((), ())), preferred_element_type=jnp.float32
    ).astype(jnp.bfloat16)
    returned = lax.all_to_all(
        produced.reshape(-1, capacity, model_width),
        "expert",
        split_axis=0,
        concat_axis=0,
        tiled=True,
    )
    returned_rows = returned.reshape(-1, model_width)
    picked = returned_rows[cell_index]
    routed_sum = jnp.sum(gate_values[:, :, None] * picked.astype(jnp.float32), axis=1)
    layer_out = (residual + routed_sum).astype(jnp.bfloat16)
    return layer_out[None]


def solution(mesh):
    in_specs = (
        P("expert", "seq", None),
        P("expert", "seq", None),
        P("expert", "seq", None),
        P(None, "seq", None),
        P("expert", None),
        P("expert", None),
        P(),
        P(None, "expert"),
        P(),
        P(),
        P("expert", "seq", None),
        P("expert", "seq", None),
        P("expert", "seq", None),
    )
    out_specs = P("expert", "seq", None)
    return jax.shard_map(functools.partial(local, seq_count=mesh.shape["seq"]), mesh=mesh, in_specs=in_specs, out_specs=out_specs, check_vma=False)
```

```python
import functools

import jax
import jax.numpy as jnp
from jax import lax
from jax.sharding import PartitionSpec as P

qk_scale = 192.0 ** (-0.5)
big_negative = -1e30


def request_of(positions, request_ends):
    return jnp.sum((positions[:, None] >= request_ends[None, :]).astype(jnp.int32), axis=1)


def merge_scores(running, scores, allowed, values):
    running_max, running_sum, running_acc = running
    new_max = jnp.maximum(running_max, jnp.max(jnp.where(allowed, scores, big_negative), axis=2))
    weights = jnp.where(allowed, jnp.exp(scores - new_max[:, :, None]), 0.0)
    new_sum = jnp.sum(weights, axis=2)
    new_acc = jnp.einsum(
        "thn,nl->thl", weights.astype(jnp.bfloat16), values, preferred_element_type=jnp.float32
    )
    return (new_max, new_sum, new_acc)


def local(
    hidden,
    queries,
    suffix_latent,
    prefix_latent,
    lengths,
    prefix_of,
    value_up,
    out_proj,
    norm_gain,
    router,
    routes,
    expert_in,
    expert_out,
    seq_count=1,
):
    local_tokens = hidden.shape[1]
    model_width = hidden.shape[2]
    key_width = suffix_latent.shape[2]
    head_count = value_up.shape[0]
    latent_width = value_up.shape[1]
    expert_count = router.shape[1]
    top_count = routes.shape[2]
    capacity = 4 * local_tokens * top_count // (3 * expert_count)
    request_count = lengths.shape[1]
    request_ends = jnp.cumsum(lengths[0])
    my_positions = lax.axis_index("seq") * local_tokens + jnp.arange(local_tokens, dtype=jnp.int32)
    my_requests = request_of(my_positions, request_ends)
    request_ids = jnp.arange(request_count, dtype=jnp.int32)
    chosen = jnp.sum(
        jnp.where(my_requests[:, None] == request_ids[None, :], prefix_of[0][None, :], 0), axis=1
    )
    prefix_pick = chosen[:, None] == jnp.arange(2, dtype=jnp.int32)[None, :]
    single_prefix = jnp.all(chosen == chosen[0])
    my_prefix = chosen[0]
    query_rows = queries[0].reshape(local_tokens, head_count, key_width)
    start_state = (
        jnp.full((local_tokens, head_count), big_negative, jnp.float32),
        jnp.zeros((local_tokens, head_count), jnp.float32),
        jnp.zeros((local_tokens, head_count, latent_width), jnp.float32),
    )
    key_stack = jnp.concatenate([suffix_latent, prefix_latent], axis=0)
    key_stack = lax.all_gather(key_stack, "seq", axis=1, tiled=True)
    suffix_piece = key_stack[:1]
    prefix_piece = key_stack[1:]
    piece_rows = suffix_piece.shape[1]
    suffix_keys = suffix_piece[0]
    key_positions = jnp.arange(piece_rows, dtype=jnp.int32)
    key_requests = request_of(key_positions, request_ends)
    suffix_allowed = (key_requests[None, :] == my_requests[:, None]) & (
        key_positions[None, :] <= my_positions[:, None]
    )
    suffix_scores = (
        jnp.einsum("thk,nk->thn", query_rows, suffix_keys, preferred_element_type=jnp.float32)
        * qk_scale
    )

    def one_prefix(running_state):
        chosen_keys = lax.dynamic_index_in_dim(prefix_piece, my_prefix, 0, keepdims=False)
        prefix_scores = (
            jnp.einsum("thk,nk->thn", query_rows, chosen_keys, preferred_element_type=jnp.float32)
            * qk_scale
        )
        scores = jnp.concatenate([suffix_scores, prefix_scores], axis=2)
        every_key = jnp.ones((local_tokens, piece_rows), dtype=bool)
        allowed = jnp.concatenate([suffix_allowed, every_key], axis=1)[:, None, :]
        values = jnp.concatenate(
            [suffix_keys[:, :latent_width], chosen_keys[:, :latent_width]], axis=0
        )
        return merge_scores(running_state, scores, allowed, values)

    def two_prefixes(running_state):
        prefix_scores = (
            jnp.einsum(
                "thk,pnk->thpn", query_rows, prefix_piece, preferred_element_type=jnp.float32
            )
            * qk_scale
        )
        scores = jnp.concatenate(
            [suffix_scores, prefix_scores.reshape(local_tokens, head_count, 2 * piece_rows)], axis=2
        )
        prefix_allowed = jnp.broadcast_to(
            prefix_pick[:, :, None], (local_tokens, 2, piece_rows)
        ).reshape(local_tokens, 2 * piece_rows)
        allowed = jnp.concatenate([suffix_allowed, prefix_allowed], axis=1)[:, None, :]
        values = jnp.concatenate(
            [
                suffix_keys[:, :latent_width],
                prefix_piece[:, :, :latent_width].reshape(2 * piece_rows, latent_width),
            ],
            axis=0,
        )
        return merge_scores(running_state, scores, allowed, values)

    final_max, final_sum, final_acc = lax.cond(single_prefix, one_prefix, two_prefixes, start_state)
    latent_out = (final_acc / final_sum[:, :, None]).astype(jnp.bfloat16)
    value_out = jnp.einsum(
        "thl,hlv->thv", latent_out, value_up, preferred_element_type=jnp.float32
    ).astype(jnp.bfloat16)
    value_out = value_out.reshape(local_tokens, head_count * value_up.shape[2])
    expert_devices = model_width // out_proj.shape[1]
    half_rows = out_proj.shape[0] // 2
    core = lax.axis_index("seq") % 2
    my_rows = lax.dynamic_slice_in_dim(out_proj, core * half_rows, half_rows, axis=0)
    my_blocks = lax.all_to_all(
        jnp.broadcast_to(my_rows[None], (expert_devices,) + my_rows.shape),
        "expert",
        split_axis=0,
        concat_axis=0,
        tiled=True,
    )
    my_blocks, value_out = lax.optimization_barrier((my_blocks, value_out))
    other_blocks = lax.ppermute(
        my_blocks, "seq", perm=[(i, i ^ 1) for i in range(seq_count)]
    )
    my_part = lax.dynamic_slice_in_dim(value_out, core * half_rows, half_rows, axis=1)
    other_part = lax.dynamic_slice_in_dim(value_out, (1 - core) * half_rows, half_rows, axis=1)
    projected = (
        jnp.einsum("tr,jrc->tjc", my_part, my_blocks, preferred_element_type=jnp.float32)
        + jnp.einsum("tr,jrc->tjc", other_part, other_blocks, preferred_element_type=jnp.float32)
    ).reshape(local_tokens, model_width)
    residual = hidden[0].astype(jnp.float32) + projected
    normed = (
        residual
        * lax.rsqrt(jnp.mean(residual * residual, axis=1, keepdims=True) + 1e-06)
        * norm_gain
    ).astype(jnp.bfloat16)
    logits = jnp.dot(normed, router, preferred_element_type=jnp.float32)
    expert_probs = jax.nn.softmax(logits, axis=1)
    expert_ids = jnp.arange(expert_count, dtype=jnp.int32)
    my_routes = routes[0]
    matches = my_routes[:, :, None] == expert_ids[None, None, :]
    gate_values = jnp.sum(jnp.where(matches, expert_probs[:, None, :], 0.0), axis=2)
    flat_hits = matches.reshape(local_tokens * top_count, expert_count).astype(jnp.int32)
    earlier = jnp.cumsum(flat_hits, axis=0) - flat_hits
    slot_index = jnp.sum(earlier * flat_hits, axis=1).reshape(local_tokens, top_count)
    cell_index = my_routes * capacity + slot_index
    cell_ids = jnp.arange(expert_count * capacity, dtype=jnp.int32)
    placing = jnp.sum(
        (cell_ids[:, None, None] == cell_index[None, :, :]).astype(jnp.int32), axis=2
    ).astype(jnp.bfloat16)
    outgoing = jnp.dot(placing, normed, preferred_element_type=jnp.float32).astype(jnp.bfloat16)
    outgoing = outgoing.reshape(expert_count, capacity, model_width)
    incoming = lax.all_to_all(outgoing, "expert", split_axis=0, concat_axis=0, tiled=True)
    in_width = expert_in.shape[2]
    full_both = lax.all_gather(
        jnp.concatenate([expert_in, expert_out], axis=2), "seq", axis=1, tiled=True
    )
    full_in, full_out = full_both[:, :, :in_width], full_both[:, :, in_width:]
    all_rows = incoming.reshape(-1, model_width)
    gate_up = jnp.dot(all_rows, full_in[0], preferred_element_type=jnp.float32)
    hidden_units = gate_up.shape[1] // 2
    active = (jax.nn.silu(gate_up[:, :hidden_units]) * gate_up[:, hidden_units:]).astype(
        jnp.bfloat16
    )
    produced = lax.dot_general(
        active, full_out[0], (((1,), (1,)), ((), ())), preferred_element_type=jnp.float32
    ).astype(jnp.bfloat16)
    returned = lax.all_to_all(
        produced.reshape(-1, capacity, model_width),
        "expert",
        split_axis=0,
        concat_axis=0,
        tiled=True,
    )
    returned_rows = returned.reshape(-1, model_width)
    combining = jnp.sum(
        jnp.where(cell_index[:, :, None] == cell_ids[None, None, :], gate_values[:, :, None], 0.0),
        axis=1,
    )
    routed_sum = jnp.dot(
        combining,
        returned_rows.astype(jnp.float32),
        precision=lax.Precision.HIGHEST,
        preferred_element_type=jnp.float32,
    )
    layer_out = (residual + routed_sum).astype(jnp.bfloat16)
    return layer_out[None]


def solution(mesh):
    in_specs = (
        P("expert", "seq", None),
        P("expert", "seq", None),
        P("expert", "seq", None),
        P(None, "seq", None),
        P("expert", None),
        P("expert", None),
        P(),
        P(None, "expert"),
        P(),
        P(),
        P("expert", "seq", None),
        P("expert", "seq", None),
        P("expert", "seq", None),
    )
    out_specs = P("expert", "seq", None)
    return jax.shard_map(functools.partial(local, seq_count=mesh.shape["seq"]), mesh=mesh, in_specs=in_specs, out_specs=out_specs, check_vma=False)
```

```python
import functools

import jax
import jax.numpy as jnp
from jax import lax
from jax.sharding import PartitionSpec as P

qk_scale = 192.0 ** (-0.5)
big_negative = -1e30


def request_of(positions, request_ends):
    return jnp.sum((positions[:, None] >= request_ends[None, :]).astype(jnp.int32), axis=1)


def merge_scores(running, scores, allowed, values):
    running_max, running_sum, running_acc = running
    new_max = jnp.maximum(running_max, jnp.max(jnp.where(allowed, scores, big_negative), axis=2))
    weights = jnp.where(allowed, jnp.exp(scores - new_max[:, :, None]), 0.0)
    new_sum = jnp.sum(weights, axis=2)
    new_acc = jnp.einsum(
        "thn,nl->thl", weights.astype(jnp.bfloat16), values, preferred_element_type=jnp.float32
    )
    return (new_max, new_sum, new_acc)


def local(
    hidden,
    queries,
    suffix_latent,
    prefix_latent,
    lengths,
    prefix_of,
    value_up,
    out_proj,
    norm_gain,
    router,
    routes,
    expert_in,
    expert_out,
    seq_count=1,
):
    local_tokens = hidden.shape[1]
    model_width = hidden.shape[2]
    key_width = suffix_latent.shape[2]
    head_count = value_up.shape[0]
    latent_width = value_up.shape[1]
    expert_count = router.shape[1]
    top_count = routes.shape[2]
    capacity = 4 * local_tokens * top_count // (3 * expert_count)
    request_count = lengths.shape[1]
    request_ends = jnp.cumsum(lengths[0])
    my_positions = lax.axis_index("seq") * local_tokens + jnp.arange(local_tokens, dtype=jnp.int32)
    my_requests = request_of(my_positions, request_ends)
    request_ids = jnp.arange(request_count, dtype=jnp.int32)
    chosen = jnp.sum(
        jnp.where(my_requests[:, None] == request_ids[None, :], prefix_of[0][None, :], 0), axis=1
    )
    prefix_pick = chosen[:, None] == jnp.arange(2, dtype=jnp.int32)[None, :]
    single_prefix = jnp.all(chosen == chosen[0])
    my_prefix = chosen[0]
    query_rows = queries[0].reshape(local_tokens, head_count, key_width)
    start_state = (
        jnp.full((local_tokens, head_count), big_negative, jnp.float32),
        jnp.zeros((local_tokens, head_count), jnp.float32),
        jnp.zeros((local_tokens, head_count, latent_width), jnp.float32),
    )
    key_stack = jnp.concatenate([suffix_latent, prefix_latent], axis=0)
    key_stack = lax.all_gather(key_stack, "seq", axis=1, tiled=True)
    suffix_piece = key_stack[:1]
    prefix_piece = key_stack[1:]
    piece_rows = suffix_piece.shape[1]
    suffix_keys = suffix_piece[0]
    key_positions = jnp.arange(piece_rows, dtype=jnp.int32)
    key_requests = request_of(key_positions, request_ends)
    suffix_allowed = (key_requests[None, :] == my_requests[:, None]) & (
        key_positions[None, :] <= my_positions[:, None]
    )
    suffix_scores = (
        jnp.einsum("thk,nk->thn", query_rows, suffix_keys, preferred_element_type=jnp.float32)
        * qk_scale
    )

    def one_prefix(running_state):
        chosen_keys = lax.dynamic_index_in_dim(prefix_piece, my_prefix, 0, keepdims=False)
        prefix_scores = (
            jnp.einsum("thk,nk->thn", query_rows, chosen_keys, preferred_element_type=jnp.float32)
            * qk_scale
        )
        scores = jnp.concatenate([suffix_scores, prefix_scores], axis=2)
        every_key = jnp.ones((local_tokens, piece_rows), dtype=bool)
        allowed = jnp.concatenate([suffix_allowed, every_key], axis=1)[:, None, :]
        values = jnp.concatenate(
            [suffix_keys[:, :latent_width], chosen_keys[:, :latent_width]], axis=0
        )
        return merge_scores(running_state, scores, allowed, values)

    def two_prefixes(running_state):
        prefix_scores = (
            jnp.einsum(
                "thk,pnk->thpn", query_rows, prefix_piece, preferred_element_type=jnp.float32
            )
            * qk_scale
        )
        scores = jnp.concatenate(
            [suffix_scores, prefix_scores.reshape(local_tokens, head_count, 2 * piece_rows)], axis=2
        )
        prefix_allowed = jnp.broadcast_to(
            prefix_pick[:, :, None], (local_tokens, 2, piece_rows)
        ).reshape(local_tokens, 2 * piece_rows)
        allowed = jnp.concatenate([suffix_allowed, prefix_allowed], axis=1)[:, None, :]
        values = jnp.concatenate(
            [
                suffix_keys[:, :latent_width],
                prefix_piece[:, :, :latent_width].reshape(2 * piece_rows, latent_width),
            ],
            axis=0,
        )
        return merge_scores(running_state, scores, allowed, values)

    final_max, final_sum, final_acc = lax.cond(single_prefix, one_prefix, two_prefixes, start_state)
    latent_out = (final_acc / final_sum[:, :, None]).astype(jnp.bfloat16)
    value_out = jnp.einsum(
        "thl,hlv->thv", latent_out, value_up, preferred_element_type=jnp.float32
    ).astype(jnp.bfloat16)
    value_out = value_out.reshape(local_tokens, head_count * value_up.shape[2])
    expert_devices = model_width // out_proj.shape[1]
    half_rows = out_proj.shape[0] // 2
    core = lax.axis_index("seq") % 2
    my_rows = lax.dynamic_slice_in_dim(out_proj, core * half_rows, half_rows, axis=0)
    my_blocks = lax.all_to_all(
        jnp.broadcast_to(my_rows[None], (expert_devices,) + my_rows.shape),
        "expert",
        split_axis=0,
        concat_axis=0,
        tiled=True,
    )
    my_blocks, value_out = lax.optimization_barrier((my_blocks, value_out))
    other_blocks = lax.ppermute(
        my_blocks, "seq", perm=[(i, i ^ 1) for i in range(seq_count)]
    )
    my_part = lax.dynamic_slice_in_dim(value_out, core * half_rows, half_rows, axis=1)
    other_part = lax.dynamic_slice_in_dim(value_out, (1 - core) * half_rows, half_rows, axis=1)
    projected = (
        jnp.einsum("tr,jrc->tjc", my_part, my_blocks, preferred_element_type=jnp.float32)
        + jnp.einsum("tr,jrc->tjc", other_part, other_blocks, preferred_element_type=jnp.float32)
    ).reshape(local_tokens, model_width)
    residual = hidden[0].astype(jnp.float32) + projected
    normed = (
        residual
        * lax.rsqrt(jnp.mean(residual * residual, axis=1, keepdims=True) + 1e-06)
        * norm_gain
    ).astype(jnp.bfloat16)
    logits = jnp.dot(normed, router, preferred_element_type=jnp.float32)
    expert_probs = jax.nn.softmax(logits, axis=1)
    expert_ids = jnp.arange(expert_count, dtype=jnp.int32)
    my_routes = routes[0]
    matches = my_routes[:, :, None] == expert_ids[None, None, :]
    gate_values = jnp.sum(jnp.where(matches, expert_probs[:, None, :], 0.0), axis=2)
    flat_hits = matches.reshape(local_tokens * top_count, expert_count).astype(jnp.int32)
    earlier = jnp.cumsum(flat_hits, axis=0) - flat_hits
    slot_index = jnp.sum(earlier * flat_hits, axis=1).reshape(local_tokens, top_count)
    cell_index = my_routes * capacity + slot_index
    cell_ids = jnp.arange(expert_count * capacity, dtype=jnp.int32)
    placing = jnp.sum(
        (cell_ids[:, None, None] == cell_index[None, :, :]).astype(jnp.int32), axis=2
    ).astype(jnp.bfloat16)
    outgoing = jnp.dot(placing, normed, preferred_element_type=jnp.float32).astype(jnp.bfloat16)
    outgoing = outgoing.reshape(expert_count, capacity, model_width)
    in_width = expert_in.shape[2]
    full_both = lax.all_gather(
        jnp.concatenate([expert_in, expert_out], axis=2), "seq", axis=1, tiled=True
    )
    full_in, full_out = full_both[:, :, :in_width], full_both[:, :, in_width:]
    combining = jnp.sum(
        jnp.where(cell_index[:, :, None] == cell_ids[None, None, :], gate_values[:, :, None], 0.0),
        axis=1,
    ).reshape(local_tokens, expert_count, capacity)
    chunk_count = 2
    chunk_slots = capacity // chunk_count
    routed_parts = []
    for chunk in range(chunk_count):
        slots = slice(chunk * chunk_slots, (chunk + 1) * chunk_slots)
        incoming = lax.all_to_all(
            outgoing[:, slots], "expert", split_axis=0, concat_axis=0, tiled=True
        )
        all_rows = incoming.reshape(-1, model_width)
        gate_up = jnp.dot(all_rows, full_in[0], preferred_element_type=jnp.float32)
        hidden_units = gate_up.shape[1] // 2
        active = (jax.nn.silu(gate_up[:, :hidden_units]) * gate_up[:, hidden_units:]).astype(
            jnp.bfloat16
        )
        produced = lax.dot_general(
            active, full_out[0], (((1,), (1,)), ((), ())), preferred_element_type=jnp.float32
        ).astype(jnp.bfloat16)
        returned = lax.all_to_all(
            produced.reshape(expert_count, chunk_slots, model_width),
            "expert",
            split_axis=0,
            concat_axis=0,
            tiled=True,
        )
        routed_parts.append(
            jnp.dot(
                combining[:, :, slots].reshape(local_tokens, expert_count * chunk_slots),
                returned.reshape(-1, model_width).astype(jnp.float32),
                precision=lax.Precision.HIGHEST,
                preferred_element_type=jnp.float32,
            )
        )
    routed_sum = routed_parts[0]
    for part in routed_parts[1:]:
        routed_sum = routed_sum + part
    layer_out = (residual + routed_sum).astype(jnp.bfloat16)
    return layer_out[None]


def solution(mesh):
    in_specs = (
        P("expert", "seq", None),
        P("expert", "seq", None),
        P("expert", "seq", None),
        P(None, "seq", None),
        P("expert", None),
        P("expert", None),
        P(),
        P(None, "expert"),
        P(),
        P(),
        P("expert", "seq", None),
        P("expert", "seq", None),
        P("expert", "seq", None),
    )
    out_specs = P("expert", "seq", None)
    return jax.shard_map(functools.partial(local, seq_count=mesh.shape["seq"]), mesh=mesh, in_specs=in_specs, out_specs=out_specs, check_vma=False)
```

```python
import functools

import jax
import jax.numpy as jnp
from jax import lax
from jax.sharding import PartitionSpec as P

qk_scale = 192.0 ** (-0.5)
big_negative = -1e30


def request_of(positions, request_ends):
    return jnp.sum((positions[:, None] >= request_ends[None, :]).astype(jnp.int32), axis=1)


def merge_scores(running, scores, allowed, values):
    running_max, running_sum, running_acc = running
    new_max = jnp.maximum(running_max, jnp.max(jnp.where(allowed, scores, big_negative), axis=2))
    weights = jnp.where(allowed, jnp.exp(scores - new_max[:, :, None]), 0.0)
    new_sum = jnp.sum(weights, axis=2)
    new_acc = jnp.einsum(
        "thn,nl->thl", weights.astype(jnp.bfloat16), values, preferred_element_type=jnp.float32
    )
    return (new_max, new_sum, new_acc)


def local(
    hidden,
    queries,
    suffix_latent,
    prefix_latent,
    lengths,
    prefix_of,
    value_up,
    out_proj,
    norm_gain,
    router,
    routes,
    expert_in,
    expert_out,
    seq_count=1,
):
    local_tokens = hidden.shape[1]
    model_width = hidden.shape[2]
    key_width = suffix_latent.shape[2]
    head_count = value_up.shape[0]
    latent_width = value_up.shape[1]
    expert_count = router.shape[1]
    top_count = routes.shape[2]
    capacity = 4 * local_tokens * top_count // (3 * expert_count)
    request_count = lengths.shape[1]
    request_ends = jnp.cumsum(lengths[0])
    my_positions = lax.axis_index("seq") * local_tokens + jnp.arange(local_tokens, dtype=jnp.int32)
    my_requests = request_of(my_positions, request_ends)
    request_ids = jnp.arange(request_count, dtype=jnp.int32)
    chosen = jnp.sum(
        jnp.where(my_requests[:, None] == request_ids[None, :], prefix_of[0][None, :], 0), axis=1
    )
    prefix_pick = chosen[:, None] == jnp.arange(2, dtype=jnp.int32)[None, :]
    query_rows = queries[0].reshape(local_tokens, head_count, key_width)
    key_stack = jnp.concatenate([suffix_latent, prefix_latent], axis=0)
    key_stack = lax.all_gather(key_stack, "seq", axis=1, tiled=True)
    block_count, piece_rows = key_stack.shape[0], key_stack.shape[1]
    key_positions = jnp.arange(piece_rows, dtype=jnp.int32)
    key_requests = request_of(key_positions, request_ends)
    suffix_allowed = (key_requests[None, :] == my_requests[:, None]) & (
        key_positions[None, :] <= my_positions[:, None]
    )
    prefix_allowed = jnp.broadcast_to(
        prefix_pick[:, :, None], (local_tokens, block_count - 1, piece_rows)
    )
    allowed = jnp.concatenate([suffix_allowed[:, None, :], prefix_allowed], axis=1)[:, None]
    scores = (
        jnp.einsum("thk,pnk->thpn", query_rows, key_stack, preferred_element_type=jnp.float32)
        * qk_scale
    )
    final_max = jnp.max(jnp.where(allowed, scores, big_negative), axis=(2, 3))
    weights = jnp.where(allowed, jnp.exp(scores - final_max[:, :, None, None]), 0.0)
    final_sum = jnp.sum(weights, axis=(2, 3))
    final_acc = jnp.einsum(
        "thpn,pnl->thl",
        weights.astype(jnp.bfloat16),
        key_stack[:, :, :latent_width],
        preferred_element_type=jnp.float32,
    )
    latent_out = (final_acc / final_sum[:, :, None]).astype(jnp.bfloat16)
    value_out = jnp.einsum(
        "thl,hlv->thv", latent_out, value_up, preferred_element_type=jnp.float32
    ).astype(jnp.bfloat16)
    value_out = value_out.reshape(local_tokens, head_count * value_up.shape[2])
    expert_devices = model_width // out_proj.shape[1]
    half_rows = out_proj.shape[0] // 2
    core = lax.axis_index("seq") % 2
    my_rows = lax.dynamic_slice_in_dim(out_proj, core * half_rows, half_rows, axis=0)
    my_blocks = lax.all_to_all(
        jnp.broadcast_to(my_rows[None], (expert_devices,) + my_rows.shape),
        "expert",
        split_axis=0,
        concat_axis=0,
        tiled=True,
    )
    my_blocks, value_out = lax.optimization_barrier((my_blocks, value_out))
    other_blocks = lax.ppermute(
        my_blocks, "seq", perm=[(i, i ^ 1) for i in range(seq_count)]
    )
    my_part = lax.dynamic_slice_in_dim(value_out, core * half_rows, half_rows, axis=1)
    other_part = lax.dynamic_slice_in_dim(value_out, (1 - core) * half_rows, half_rows, axis=1)
    projected = (
        jnp.einsum("tr,jrc->tjc", my_part, my_blocks, preferred_element_type=jnp.float32)
        + jnp.einsum("tr,jrc->tjc", other_part, other_blocks, preferred_element_type=jnp.float32)
    ).reshape(local_tokens, model_width)
    residual = hidden[0].astype(jnp.float32) + projected
    normed = (
        residual
        * lax.rsqrt(jnp.mean(residual * residual, axis=1, keepdims=True) + 1e-06)
        * norm_gain
    ).astype(jnp.bfloat16)
    logits = jnp.dot(normed, router, preferred_element_type=jnp.float32)
    expert_probs = jax.nn.softmax(logits, axis=1)
    expert_ids = jnp.arange(expert_count, dtype=jnp.int32)
    my_routes = routes[0]
    matches = my_routes[:, :, None] == expert_ids[None, None, :]
    gate_values = jnp.sum(jnp.where(matches, expert_probs[:, None, :], 0.0), axis=2)
    flat_hits = matches.reshape(local_tokens * top_count, expert_count).astype(jnp.int32)
    earlier = jnp.cumsum(flat_hits, axis=0) - flat_hits
    slot_index = jnp.sum(earlier * flat_hits, axis=1).reshape(local_tokens, top_count)
    cell_index = my_routes * capacity + slot_index
    cell_ids = jnp.arange(expert_count * capacity, dtype=jnp.int32)
    placing = jnp.sum(
        (cell_ids[:, None, None] == cell_index[None, :, :]).astype(jnp.int32), axis=2
    ).astype(jnp.bfloat16)
    outgoing = jnp.dot(placing, normed, preferred_element_type=jnp.float32).astype(jnp.bfloat16)
    outgoing = outgoing.reshape(expert_count, capacity, model_width)
    incoming = lax.all_to_all(outgoing, "expert", split_axis=0, concat_axis=0, tiled=True)
    in_width = expert_in.shape[2]
    full_both = lax.all_gather(
        jnp.concatenate([expert_in, expert_out], axis=2), "seq", axis=1, tiled=True
    )
    full_in, full_out = full_both[:, :, :in_width], full_both[:, :, in_width:]
    all_rows = incoming.reshape(-1, model_width)
    gate_up = jnp.dot(all_rows, full_in[0], preferred_element_type=jnp.float32)
    hidden_units = gate_up.shape[1] // 2
    active = (jax.nn.silu(gate_up[:, :hidden_units]) * gate_up[:, hidden_units:]).astype(
        jnp.bfloat16
    )
    produced = lax.dot_general(
        active, full_out[0], (((1,), (1,)), ((), ())), preferred_element_type=jnp.float32
    ).astype(jnp.bfloat16)
    returned = lax.all_to_all(
        produced.reshape(-1, capacity, model_width),
        "expert",
        split_axis=0,
        concat_axis=0,
        tiled=True,
    )
    returned_rows = returned.reshape(-1, model_width)
    combining = jnp.sum(
        jnp.where(cell_index[:, :, None] == cell_ids[None, None, :], gate_values[:, :, None], 0.0),
        axis=1,
    )
    routed_sum = jnp.dot(
        combining,
        returned_rows.astype(jnp.float32),
        precision=lax.Precision.HIGHEST,
        preferred_element_type=jnp.float32,
    )
    layer_out = (residual + routed_sum).astype(jnp.bfloat16)
    return layer_out[None]


def solution(mesh):
    in_specs = (
        P("expert", "seq", None),
        P("expert", "seq", None),
        P("expert", "seq", None),
        P(None, "seq", None),
        P("expert", None),
        P("expert", None),
        P(),
        P(None, "expert"),
        P(),
        P(),
        P("expert", "seq", None),
        P("expert", "seq", None),
        P("expert", "seq", None),
    )
    out_specs = P("expert", "seq", None)
    return jax.shard_map(functools.partial(local, seq_count=mesh.shape["seq"]), mesh=mesh, in_specs=in_specs, out_specs=out_specs, check_vma=False)
```

```python
import functools

import jax
import jax.numpy as jnp
from jax import lax
from jax.sharding import PartitionSpec as P

qk_scale = 192.0 ** (-0.5)
big_negative = -1e30


def request_of(positions, request_ends):
    return jnp.sum((positions[:, None] >= request_ends[None, :]).astype(jnp.int32), axis=1)


def merge_scores(running, scores, allowed, values):
    running_max, running_sum, running_acc = running
    new_max = jnp.maximum(running_max, jnp.max(jnp.where(allowed, scores, big_negative), axis=2))
    weights = jnp.where(allowed, jnp.exp(scores - new_max[:, :, None]), 0.0)
    new_sum = jnp.sum(weights, axis=2)
    new_acc = jnp.einsum(
        "thn,nl->thl", weights.astype(jnp.bfloat16), values, preferred_element_type=jnp.float32
    )
    return (new_max, new_sum, new_acc)


def local(
    hidden,
    queries,
    suffix_latent,
    prefix_latent,
    lengths,
    prefix_of,
    value_up,
    out_proj,
    norm_gain,
    router,
    routes,
    expert_in,
    expert_out,
    seq_count=1,
):
    local_tokens = hidden.shape[1]
    model_width = hidden.shape[2]
    key_width = suffix_latent.shape[2]
    head_count = value_up.shape[0]
    latent_width = value_up.shape[1]
    expert_count = router.shape[1]
    top_count = routes.shape[2]
    capacity = 4 * local_tokens * top_count // (3 * expert_count)
    request_count = lengths.shape[1]
    request_ends = jnp.cumsum(lengths[0])
    my_positions = lax.axis_index("seq") * local_tokens + jnp.arange(local_tokens, dtype=jnp.int32)
    my_requests = request_of(my_positions, request_ends)
    request_ids = jnp.arange(request_count, dtype=jnp.int32)
    chosen = jnp.sum(
        jnp.where(my_requests[:, None] == request_ids[None, :], prefix_of[0][None, :], 0), axis=1
    )
    prefix_pick = chosen[:, None] == jnp.arange(2, dtype=jnp.int32)[None, :]
    query_rows = queries[0].reshape(local_tokens, head_count, key_width)
    key_stack = jnp.concatenate([suffix_latent, prefix_latent], axis=0)
    key_stack = lax.all_gather(key_stack, "seq", axis=1, tiled=True)
    block_count, piece_rows = key_stack.shape[0], key_stack.shape[1]
    key_positions = jnp.arange(piece_rows, dtype=jnp.int32)
    key_requests = request_of(key_positions, request_ends)
    suffix_allowed = (key_requests[None, :] == my_requests[:, None]) & (
        key_positions[None, :] <= my_positions[:, None]
    )
    prefix_allowed = jnp.broadcast_to(
        prefix_pick[:, :, None], (local_tokens, block_count - 1, piece_rows)
    )
    allowed = jnp.concatenate([suffix_allowed[:, None, :], prefix_allowed], axis=1)[:, None]
    scores = (
        jnp.einsum("thk,pnk->thpn", query_rows, key_stack, preferred_element_type=jnp.float32)
        * qk_scale
    )
    final_max = jnp.max(jnp.where(allowed, scores, big_negative), axis=(2, 3))
    weights = jnp.where(allowed, jnp.exp(scores - final_max[:, :, None, None]), 0.0)
    final_sum = jnp.sum(weights, axis=(2, 3))
    final_acc = jnp.einsum(
        "thpn,pnl->thl",
        weights.astype(jnp.bfloat16),
        key_stack[:, :, :latent_width],
        preferred_element_type=jnp.float32,
    )
    latent_out = (final_acc / final_sum[:, :, None]).astype(jnp.bfloat16)
    value_out = jnp.einsum(
        "thl,hlv->thv", latent_out, value_up, preferred_element_type=jnp.float32
    ).astype(jnp.bfloat16)
    value_out = value_out.reshape(local_tokens, head_count * value_up.shape[2])
    expert_devices = model_width // out_proj.shape[1]
    half_rows = out_proj.shape[0] // 2
    core = lax.axis_index("seq") % 2
    my_rows = lax.dynamic_slice_in_dim(out_proj, core * half_rows, half_rows, axis=0)
    my_blocks = lax.all_to_all(
        jnp.broadcast_to(my_rows[None], (expert_devices,) + my_rows.shape),
        "expert",
        split_axis=0,
        concat_axis=0,
        tiled=True,
    )
    my_blocks, value_out = lax.optimization_barrier((my_blocks, value_out))
    pair = [(i, i ^ 1) for i in range(seq_count)]
    my_part = lax.dynamic_slice_in_dim(value_out, core * half_rows, half_rows, axis=1)
    other_part = lax.dynamic_slice_in_dim(value_out, (1 - core) * half_rows, half_rows, axis=1)
    partner_part = lax.ppermute(other_part, "seq", perm=pair)
    partner_partial = jnp.einsum(
        "tr,jrc->tjc", partner_part, my_blocks, preferred_element_type=jnp.float32
    )
    projected = (
        jnp.einsum("tr,jrc->tjc", my_part, my_blocks, preferred_element_type=jnp.float32)
        + lax.ppermute(partner_partial, "seq", perm=pair)
    ).reshape(local_tokens, model_width)
    residual = hidden[0].astype(jnp.float32) + projected
    normed = (
        residual
        * lax.rsqrt(jnp.mean(residual * residual, axis=1, keepdims=True) + 1e-06)
        * norm_gain
    ).astype(jnp.bfloat16)
    logits = jnp.dot(normed, router, preferred_element_type=jnp.float32)
    expert_probs = jax.nn.softmax(logits, axis=1)
    expert_ids = jnp.arange(expert_count, dtype=jnp.int32)
    my_routes = routes[0]
    matches = my_routes[:, :, None] == expert_ids[None, None, :]
    gate_values = jnp.sum(jnp.where(matches, expert_probs[:, None, :], 0.0), axis=2)
    flat_hits = matches.reshape(local_tokens * top_count, expert_count).astype(jnp.int32)
    earlier = jnp.cumsum(flat_hits, axis=0) - flat_hits
    slot_index = jnp.sum(earlier * flat_hits, axis=1).reshape(local_tokens, top_count)
    cell_index = my_routes * capacity + slot_index
    cell_ids = jnp.arange(expert_count * capacity, dtype=jnp.int32)
    placing = jnp.sum(
        (cell_ids[:, None, None] == cell_index[None, :, :]).astype(jnp.int32), axis=2
    ).astype(jnp.bfloat16)
    outgoing = jnp.dot(placing, normed, preferred_element_type=jnp.float32).astype(jnp.bfloat16)
    outgoing = outgoing.reshape(expert_count, capacity, model_width)
    incoming = lax.all_to_all(outgoing, "expert", split_axis=0, concat_axis=0, tiled=True)
    in_width = expert_in.shape[2]
    full_both = lax.all_gather(
        jnp.concatenate([expert_in, expert_out], axis=2), "seq", axis=1, tiled=True
    )
    full_in, full_out = full_both[:, :, :in_width], full_both[:, :, in_width:]
    all_rows = incoming.reshape(-1, model_width)
    gate_up = jnp.dot(all_rows, full_in[0], preferred_element_type=jnp.float32)
    hidden_units = gate_up.shape[1] // 2
    active = (jax.nn.silu(gate_up[:, :hidden_units]) * gate_up[:, hidden_units:]).astype(
        jnp.bfloat16
    )
    produced = lax.dot_general(
        active, full_out[0], (((1,), (1,)), ((), ())), preferred_element_type=jnp.float32
    ).astype(jnp.bfloat16)
    returned = lax.all_to_all(
        produced.reshape(-1, capacity, model_width),
        "expert",
        split_axis=0,
        concat_axis=0,
        tiled=True,
    )
    returned_rows = returned.reshape(-1, model_width)
    combining = jnp.sum(
        jnp.where(cell_index[:, :, None] == cell_ids[None, None, :], gate_values[:, :, None], 0.0),
        axis=1,
    )
    routed_sum = jnp.dot(
        combining,
        returned_rows.astype(jnp.float32),
        precision=lax.Precision.HIGHEST,
        preferred_element_type=jnp.float32,
    )
    layer_out = (residual + routed_sum).astype(jnp.bfloat16)
    return layer_out[None]


def solution(mesh):
    in_specs = (
        P("expert", "seq", None),
        P("expert", "seq", None),
        P("expert", "seq", None),
        P(None, "seq", None),
        P("expert", None),
        P("expert", None),
        P(),
        P(None, "expert"),
        P(),
        P(),
        P("expert", "seq", None),
        P("expert", "seq", None),
        P("expert", "seq", None),
    )
    out_specs = P("expert", "seq", None)
    return jax.shard_map(functools.partial(local, seq_count=mesh.shape["seq"]), mesh=mesh, in_specs=in_specs, out_specs=out_specs, check_vma=False)
```

```python
import functools

import jax
import jax.numpy as jnp
from jax import lax
from jax.sharding import PartitionSpec as P

qk_scale = 192.0 ** (-0.5)
big_negative = -1e30


def request_of(positions, request_ends):
    return jnp.sum((positions[:, None] >= request_ends[None, :]).astype(jnp.int32), axis=1)


def merge_scores(running, scores, allowed, values):
    running_max, running_sum, running_acc = running
    new_max = jnp.maximum(running_max, jnp.max(jnp.where(allowed, scores, big_negative), axis=2))
    weights = jnp.where(allowed, jnp.exp(scores - new_max[:, :, None]), 0.0)
    new_sum = jnp.sum(weights, axis=2)
    new_acc = jnp.einsum(
        "thn,nl->thl", weights.astype(jnp.bfloat16), values, preferred_element_type=jnp.float32
    )
    return (new_max, new_sum, new_acc)


def local(
    hidden,
    queries,
    suffix_latent,
    prefix_latent,
    lengths,
    prefix_of,
    value_up,
    out_proj,
    norm_gain,
    router,
    routes,
    expert_in,
    expert_out,
    seq_count=1,
):
    local_tokens = hidden.shape[1]
    model_width = hidden.shape[2]
    key_width = suffix_latent.shape[2]
    head_count = value_up.shape[0]
    latent_width = value_up.shape[1]
    expert_count = router.shape[1]
    top_count = routes.shape[2]
    capacity = 4 * local_tokens * top_count // (3 * expert_count)
    request_count = lengths.shape[1]
    request_ends = jnp.cumsum(lengths[0])
    my_positions = lax.axis_index("seq") * local_tokens + jnp.arange(local_tokens, dtype=jnp.int32)
    my_requests = request_of(my_positions, request_ends)
    request_ids = jnp.arange(request_count, dtype=jnp.int32)
    chosen = jnp.sum(
        jnp.where(my_requests[:, None] == request_ids[None, :], prefix_of[0][None, :], 0), axis=1
    )
    prefix_pick = chosen[:, None] == jnp.arange(2, dtype=jnp.int32)[None, :]
    query_rows = queries[0].reshape(local_tokens, head_count, key_width)
    key_stack = jnp.concatenate([suffix_latent, prefix_latent], axis=0)
    key_stack = lax.all_gather(key_stack, "seq", axis=1, tiled=True)
    block_count, piece_rows = key_stack.shape[0], key_stack.shape[1]
    key_positions = jnp.arange(piece_rows, dtype=jnp.int32)
    key_requests = request_of(key_positions, request_ends)
    suffix_allowed = (key_requests[None, :] == my_requests[:, None]) & (
        key_positions[None, :] <= my_positions[:, None]
    )
    prefix_allowed = jnp.broadcast_to(
        prefix_pick[:, :, None], (local_tokens, block_count - 1, piece_rows)
    )
    allowed = jnp.concatenate([suffix_allowed[:, None, :], prefix_allowed], axis=1)
    allowed = allowed.reshape(local_tokens, 1, block_count * piece_rows)
    every_key = key_stack.reshape(block_count * piece_rows, key_width)
    scores = (
        jnp.einsum("thk,nk->thn", query_rows, every_key, preferred_element_type=jnp.float32)
        * qk_scale
    )
    final_max = jnp.max(jnp.where(allowed, scores, big_negative), axis=2)
    weights = jnp.where(allowed, jnp.exp(scores - final_max[:, :, None]), 0.0)
    final_sum = jnp.sum(weights, axis=2)
    final_acc = jnp.einsum(
        "thn,nl->thl",
        weights.astype(jnp.bfloat16),
        every_key[:, :latent_width],
        preferred_element_type=jnp.float32,
    )
    latent_out = (final_acc / final_sum[:, :, None]).astype(jnp.bfloat16)
    value_out = jnp.einsum(
        "thl,hlv->thv", latent_out, value_up, preferred_element_type=jnp.float32
    ).astype(jnp.bfloat16)
    value_out = value_out.reshape(local_tokens, head_count * value_up.shape[2])
    expert_devices = model_width // out_proj.shape[1]
    half_rows = out_proj.shape[0] // 2
    core = lax.axis_index("seq") % 2
    my_rows = lax.dynamic_slice_in_dim(out_proj, core * half_rows, half_rows, axis=0)
    my_blocks = lax.all_to_all(
        jnp.broadcast_to(my_rows[None], (expert_devices,) + my_rows.shape),
        "expert",
        split_axis=0,
        concat_axis=0,
        tiled=True,
    )
    my_blocks, value_out = lax.optimization_barrier((my_blocks, value_out))
    pair = [(i, i ^ 1) for i in range(seq_count)]
    my_part = lax.dynamic_slice_in_dim(value_out, core * half_rows, half_rows, axis=1)
    other_part = lax.dynamic_slice_in_dim(value_out, (1 - core) * half_rows, half_rows, axis=1)
    partner_part = lax.ppermute(other_part, "seq", perm=pair)
    partner_partial = jnp.einsum(
        "tr,jrc->tjc", partner_part, my_blocks, preferred_element_type=jnp.float32
    )
    projected = (
        jnp.einsum("tr,jrc->tjc", my_part, my_blocks, preferred_element_type=jnp.float32)
        + lax.ppermute(partner_partial, "seq", perm=pair)
    ).reshape(local_tokens, model_width)
    residual = hidden[0].astype(jnp.float32) + projected
    normed = (
        residual
        * lax.rsqrt(jnp.mean(residual * residual, axis=1, keepdims=True) + 1e-06)
        * norm_gain
    ).astype(jnp.bfloat16)
    logits = jnp.dot(normed, router, preferred_element_type=jnp.float32)
    expert_probs = jax.nn.softmax(logits, axis=1)
    expert_ids = jnp.arange(expert_count, dtype=jnp.int32)
    my_routes = routes[0]
    matches = my_routes[:, :, None] == expert_ids[None, None, :]
    gate_values = jnp.sum(jnp.where(matches, expert_probs[:, None, :], 0.0), axis=2)
    flat_hits = matches.reshape(local_tokens * top_count, expert_count).astype(jnp.int32)
    earlier = jnp.cumsum(flat_hits, axis=0) - flat_hits
    slot_index = jnp.sum(earlier * flat_hits, axis=1).reshape(local_tokens, top_count)
    cell_index = my_routes * capacity + slot_index
    cell_ids = jnp.arange(expert_count * capacity, dtype=jnp.int32)
    placing = jnp.sum(
        (cell_ids[:, None, None] == cell_index[None, :, :]).astype(jnp.int32), axis=2
    ).astype(jnp.bfloat16)
    outgoing = jnp.dot(placing, normed, preferred_element_type=jnp.float32).astype(jnp.bfloat16)
    outgoing = outgoing.reshape(expert_count, capacity, model_width)
    incoming = lax.all_to_all(outgoing, "expert", split_axis=0, concat_axis=0, tiled=True)
    in_width = expert_in.shape[2]
    full_both = lax.all_gather(
        jnp.concatenate([expert_in, expert_out], axis=2), "seq", axis=1, tiled=True
    )
    full_in, full_out = full_both[:, :, :in_width], full_both[:, :, in_width:]
    all_rows = incoming.reshape(-1, model_width)
    gate_up = jnp.dot(all_rows, full_in[0], preferred_element_type=jnp.float32)
    hidden_units = gate_up.shape[1] // 2
    active = (jax.nn.silu(gate_up[:, :hidden_units]) * gate_up[:, hidden_units:]).astype(
        jnp.bfloat16
    )
    produced = lax.dot_general(
        active, full_out[0], (((1,), (1,)), ((), ())), preferred_element_type=jnp.float32
    ).astype(jnp.bfloat16)
    returned = lax.all_to_all(
        produced.reshape(-1, capacity, model_width),
        "expert",
        split_axis=0,
        concat_axis=0,
        tiled=True,
    )
    returned_rows = returned.reshape(-1, model_width)
    combining = jnp.sum(
        jnp.where(cell_index[:, :, None] == cell_ids[None, None, :], gate_values[:, :, None], 0.0),
        axis=1,
    )
    routed_sum = jnp.dot(
        combining,
        returned_rows.astype(jnp.float32),
        precision=lax.Precision.HIGHEST,
        preferred_element_type=jnp.float32,
    )
    layer_out = (residual + routed_sum).astype(jnp.bfloat16)
    return layer_out[None]


def solution(mesh):
    in_specs = (
        P("expert", "seq", None),
        P("expert", "seq", None),
        P("expert", "seq", None),
        P(None, "seq", None),
        P("expert", None),
        P("expert", None),
        P(),
        P(None, "expert"),
        P(),
        P(),
        P("expert", "seq", None),
        P("expert", "seq", None),
        P("expert", "seq", None),
    )
    out_specs = P("expert", "seq", None)
    return jax.shard_map(functools.partial(local, seq_count=mesh.shape["seq"]), mesh=mesh, in_specs=in_specs, out_specs=out_specs, check_vma=False)
```

```python
import functools

import jax
import jax.numpy as jnp
from jax import lax
from jax.sharding import PartitionSpec as P

qk_scale = 192.0 ** (-0.5)
big_negative = -1e30


def request_of(positions, request_ends):
    return jnp.sum((positions[:, None] >= request_ends[None, :]).astype(jnp.int32), axis=1)


def merge_scores(running, scores, allowed, values):
    running_max, running_sum, running_acc = running
    new_max = jnp.maximum(running_max, jnp.max(jnp.where(allowed, scores, big_negative), axis=2))
    weights = jnp.where(allowed, jnp.exp(scores - new_max[:, :, None]), 0.0)
    new_sum = jnp.sum(weights, axis=2)
    new_acc = jnp.einsum(
        "thn,nl->thl", weights.astype(jnp.bfloat16), values, preferred_element_type=jnp.float32
    )
    return (new_max, new_sum, new_acc)


def local(
    hidden,
    queries,
    suffix_latent,
    prefix_latent,
    lengths,
    prefix_of,
    value_up,
    out_proj,
    norm_gain,
    router,
    routes,
    expert_in,
    expert_out,
    seq_count=1,
):
    local_tokens = hidden.shape[1]
    model_width = hidden.shape[2]
    key_width = suffix_latent.shape[2]
    head_count = value_up.shape[0]
    latent_width = value_up.shape[1]
    expert_count = router.shape[1]
    top_count = routes.shape[2]
    capacity = 4 * local_tokens * top_count // (3 * expert_count)
    request_count = lengths.shape[1]
    request_ends = jnp.cumsum(lengths[0])
    my_positions = lax.axis_index("seq") * local_tokens + jnp.arange(local_tokens, dtype=jnp.int32)
    my_requests = request_of(my_positions, request_ends)
    request_ids = jnp.arange(request_count, dtype=jnp.int32)
    chosen = jnp.sum(
        jnp.where(my_requests[:, None] == request_ids[None, :], prefix_of[0][None, :], 0), axis=1
    )
    prefix_pick = chosen[:, None] == jnp.arange(2, dtype=jnp.int32)[None, :]
    query_rows = queries[0].reshape(local_tokens, head_count, key_width)
    key_stack = jnp.concatenate([suffix_latent, prefix_latent], axis=0)
    key_stack = lax.all_gather(key_stack, "seq", axis=1, tiled=True)
    block_count, piece_rows = key_stack.shape[0], key_stack.shape[1]
    key_positions = jnp.arange(piece_rows, dtype=jnp.int32)
    key_requests = request_of(key_positions, request_ends)
    suffix_allowed = (key_requests[None, :] == my_requests[:, None]) & (
        key_positions[None, :] <= my_positions[:, None]
    )
    prefix_allowed = jnp.broadcast_to(
        prefix_pick[:, :, None], (local_tokens, block_count - 1, piece_rows)
    )
    allowed = jnp.concatenate([suffix_allowed[:, None, :], prefix_allowed], axis=1)
    allowed = allowed.reshape(local_tokens, 1, block_count * piece_rows)
    every_key = key_stack.reshape(block_count * piece_rows, key_width)
    scores = (
        jnp.einsum("thk,nk->thn", query_rows, every_key, preferred_element_type=jnp.float32)
        * qk_scale
    )
    final_max = jnp.max(jnp.where(allowed, scores, big_negative), axis=2)
    expert_devices = model_width // out_proj.shape[1]
    half_rows = out_proj.shape[0] // 2
    core = lax.axis_index("seq") % 2
    my_rows = lax.dynamic_slice_in_dim(out_proj, core * half_rows, half_rows, axis=0)
    my_blocks = lax.all_to_all(
        jnp.broadcast_to(my_rows[None], (expert_devices,) + my_rows.shape),
        "expert",
        split_axis=0,
        concat_axis=0,
        tiled=True,
    )
    my_blocks, final_max = lax.optimization_barrier((my_blocks, final_max))
    weights = jnp.where(allowed, jnp.exp(scores - final_max[:, :, None]), 0.0)
    final_sum = jnp.sum(weights, axis=2)
    final_acc = jnp.einsum(
        "thn,nl->thl",
        weights.astype(jnp.bfloat16),
        every_key[:, :latent_width],
        preferred_element_type=jnp.float32,
    )
    latent_out = (final_acc / final_sum[:, :, None]).astype(jnp.bfloat16)
    value_out = jnp.einsum(
        "thl,hlv->thv", latent_out, value_up, preferred_element_type=jnp.float32
    ).astype(jnp.bfloat16)
    value_out = value_out.reshape(local_tokens, head_count * value_up.shape[2])
    pair = [(i, i ^ 1) for i in range(seq_count)]
    other_blocks = lax.ppermute(my_blocks, "seq", perm=pair)
    my_part = lax.dynamic_slice_in_dim(value_out, core * half_rows, half_rows, axis=1)
    other_part = lax.dynamic_slice_in_dim(value_out, (1 - core) * half_rows, half_rows, axis=1)
    projected = (
        jnp.einsum("tr,jrc->tjc", my_part, my_blocks, preferred_element_type=jnp.float32)
        + jnp.einsum("tr,jrc->tjc", other_part, other_blocks, preferred_element_type=jnp.float32)
    ).reshape(local_tokens, model_width)
    residual = hidden[0].astype(jnp.float32) + projected
    normed = (
        residual
        * lax.rsqrt(jnp.mean(residual * residual, axis=1, keepdims=True) + 1e-06)
        * norm_gain
    ).astype(jnp.bfloat16)
    logits = jnp.dot(normed, router, preferred_element_type=jnp.float32)
    expert_probs = jax.nn.softmax(logits, axis=1)
    expert_ids = jnp.arange(expert_count, dtype=jnp.int32)
    my_routes = routes[0]
    matches = my_routes[:, :, None] == expert_ids[None, None, :]
    gate_values = jnp.sum(jnp.where(matches, expert_probs[:, None, :], 0.0), axis=2)
    flat_hits = matches.reshape(local_tokens * top_count, expert_count).astype(jnp.int32)
    earlier = jnp.cumsum(flat_hits, axis=0) - flat_hits
    slot_index = jnp.sum(earlier * flat_hits, axis=1).reshape(local_tokens, top_count)
    cell_index = my_routes * capacity + slot_index
    cell_ids = jnp.arange(expert_count * capacity, dtype=jnp.int32)
    placing = jnp.sum(
        (cell_ids[:, None, None] == cell_index[None, :, :]).astype(jnp.int32), axis=2
    ).astype(jnp.bfloat16)
    outgoing = jnp.dot(placing, normed, preferred_element_type=jnp.float32).astype(jnp.bfloat16)
    outgoing = outgoing.reshape(expert_count, capacity, model_width)
    incoming = lax.all_to_all(outgoing, "expert", split_axis=0, concat_axis=0, tiled=True)
    in_width = expert_in.shape[2]
    full_both = lax.all_gather(
        jnp.concatenate([expert_in, expert_out], axis=2), "seq", axis=1, tiled=True
    )
    full_in, full_out = full_both[:, :, :in_width], full_both[:, :, in_width:]
    all_rows = incoming.reshape(-1, model_width)
    gate_up = jnp.dot(all_rows, full_in[0], preferred_element_type=jnp.float32)
    hidden_units = gate_up.shape[1] // 2
    active = (jax.nn.silu(gate_up[:, :hidden_units]) * gate_up[:, hidden_units:]).astype(
        jnp.bfloat16
    )
    produced = lax.dot_general(
        active, full_out[0], (((1,), (1,)), ((), ())), preferred_element_type=jnp.float32
    ).astype(jnp.bfloat16)
    returned = lax.all_to_all(
        produced.reshape(-1, capacity, model_width),
        "expert",
        split_axis=0,
        concat_axis=0,
        tiled=True,
    )
    returned_rows = returned.reshape(-1, model_width)
    combining = jnp.sum(
        jnp.where(cell_index[:, :, None] == cell_ids[None, None, :], gate_values[:, :, None], 0.0),
        axis=1,
    )
    routed_sum = jnp.dot(
        combining,
        returned_rows.astype(jnp.float32),
        precision=lax.Precision.HIGHEST,
        preferred_element_type=jnp.float32,
    )
    layer_out = (residual + routed_sum).astype(jnp.bfloat16)
    return layer_out[None]


def solution(mesh):
    in_specs = (
        P("expert", "seq", None),
        P("expert", "seq", None),
        P("expert", "seq", None),
        P(None, "seq", None),
        P("expert", None),
        P("expert", None),
        P(),
        P(None, "expert"),
        P(),
        P(),
        P("expert", "seq", None),
        P("expert", "seq", None),
        P("expert", "seq", None),
    )
    out_specs = P("expert", "seq", None)
    return jax.shard_map(functools.partial(local, seq_count=mesh.shape["seq"]), mesh=mesh, in_specs=in_specs, out_specs=out_specs, check_vma=False)
```

```python
import functools

import jax
import jax.numpy as jnp
from jax import lax
from jax.experimental import pallas as pl
from jax.sharding import PartitionSpec as P

qk_scale = 192.0 ** (-0.5)
big_negative = -1e30


def request_of(positions, request_ends):
    return jnp.sum((positions[:, None] >= request_ends[None, :]).astype(jnp.int32), axis=1)


def merge_scores(running, scores, allowed, values):
    running_max, running_sum, running_acc = running
    new_max = jnp.maximum(running_max, jnp.max(jnp.where(allowed, scores, big_negative), axis=2))
    weights = jnp.where(allowed, jnp.exp(scores - new_max[:, :, None]), 0.0)
    new_sum = jnp.sum(weights, axis=2)
    new_acc = jnp.einsum(
        "thn,nl->thl", weights.astype(jnp.bfloat16), values, preferred_element_type=jnp.float32
    )
    return (new_max, new_sum, new_acc)


def attention_kernel(q_ref, k_ref, m_ref, o_ref, *, heads, latent_width):
    keys = k_ref[...]
    scores = (
        lax.dot_general(
            q_ref[...], keys, (((1,), (1,)), ((), ())), preferred_element_type=jnp.float32
        )
        * qk_scale
    )
    rows, count = scores.shape
    scores = scores.reshape(rows // heads, heads, count)
    allowed = m_ref[...][:, None, :] > 0.5
    top = jnp.max(jnp.where(allowed, scores, big_negative), axis=2, keepdims=True)
    weights = jnp.where(allowed, jnp.exp(scores - top), 0.0)
    total = jnp.sum(weights, axis=2, keepdims=True)
    acc = jnp.dot(
        weights.reshape(rows, count).astype(jnp.bfloat16),
        keys[:, :latent_width],
        preferred_element_type=jnp.float32,
    )
    o_ref[...] = (
        (acc.reshape(rows // heads, heads, latent_width) / total)
        .reshape(rows, latent_width)
        .astype(o_ref.dtype)
    )


def attend(query_rows, every_key, allowed, heads, latent_width):
    rows, key_width = query_rows.shape
    count = every_key.shape[0]
    flops = 2 * rows * count * (key_width + latent_width)
    return pl.pallas_call(
        functools.partial(attention_kernel, heads=heads, latent_width=latent_width),
        out_shape=jax.ShapeDtypeStruct((rows, latent_width), jnp.bfloat16),
        cost_estimate=pl.CostEstimate(
            flops=flops,
            transcendentals=rows * count,
            bytes_accessed=2 * (rows * key_width + count * key_width + rows * latent_width)
            + 4 * allowed.size,
        ),
    )(query_rows, every_key, allowed)


def local(
    hidden,
    queries,
    suffix_latent,
    prefix_latent,
    lengths,
    prefix_of,
    value_up,
    out_proj,
    norm_gain,
    router,
    routes,
    expert_in,
    expert_out,
    seq_count=1,
):
    local_tokens = hidden.shape[1]
    model_width = hidden.shape[2]
    key_width = suffix_latent.shape[2]
    head_count = value_up.shape[0]
    latent_width = value_up.shape[1]
    expert_count = router.shape[1]
    top_count = routes.shape[2]
    capacity = 4 * local_tokens * top_count // (3 * expert_count)
    request_count = lengths.shape[1]
    request_ends = jnp.cumsum(lengths[0])
    my_positions = lax.axis_index("seq") * local_tokens + jnp.arange(local_tokens, dtype=jnp.int32)
    my_requests = request_of(my_positions, request_ends)
    request_ids = jnp.arange(request_count, dtype=jnp.int32)
    chosen = jnp.sum(
        jnp.where(my_requests[:, None] == request_ids[None, :], prefix_of[0][None, :], 0), axis=1
    )
    prefix_pick = chosen[:, None] == jnp.arange(2, dtype=jnp.int32)[None, :]
    query_rows = queries[0].reshape(local_tokens, head_count, key_width)
    key_stack = jnp.concatenate([suffix_latent, prefix_latent], axis=0)
    key_stack = lax.all_gather(key_stack, "seq", axis=1, tiled=True)
    block_count, piece_rows = key_stack.shape[0], key_stack.shape[1]
    key_positions = jnp.arange(piece_rows, dtype=jnp.int32)
    key_requests = request_of(key_positions, request_ends)
    suffix_allowed = (key_requests[None, :] == my_requests[:, None]) & (
        key_positions[None, :] <= my_positions[:, None]
    )
    prefix_allowed = jnp.broadcast_to(
        prefix_pick[:, :, None], (local_tokens, block_count - 1, piece_rows)
    )
    allowed = jnp.concatenate([suffix_allowed[:, None, :], prefix_allowed], axis=1)
    allowed = allowed.reshape(local_tokens, block_count * piece_rows).astype(jnp.float32)
    every_key = key_stack.reshape(block_count * piece_rows, key_width)
    latent_out = attend(
        query_rows.reshape(local_tokens * head_count, key_width),
        every_key,
        allowed,
        head_count,
        latent_width,
    ).reshape(local_tokens, head_count, latent_width)
    value_out = jnp.einsum(
        "thl,hlv->thv", latent_out, value_up, preferred_element_type=jnp.float32
    ).astype(jnp.bfloat16)
    value_out = value_out.reshape(local_tokens, head_count * value_up.shape[2])
    expert_devices = model_width // out_proj.shape[1]
    half_rows = out_proj.shape[0] // 2
    core = lax.axis_index("seq") % 2
    my_rows = lax.dynamic_slice_in_dim(out_proj, core * half_rows, half_rows, axis=0)
    my_blocks = lax.all_to_all(
        jnp.broadcast_to(my_rows[None], (expert_devices,) + my_rows.shape),
        "expert",
        split_axis=0,
        concat_axis=0,
        tiled=True,
    )
    my_blocks, value_out = lax.optimization_barrier((my_blocks, value_out))
    pair = [(i, i ^ 1) for i in range(seq_count)]
    my_part = lax.dynamic_slice_in_dim(value_out, core * half_rows, half_rows, axis=1)
    other_part = lax.dynamic_slice_in_dim(value_out, (1 - core) * half_rows, half_rows, axis=1)
    partner_part = lax.ppermute(other_part, "seq", perm=pair)
    partner_partial = jnp.einsum(
        "tr,jrc->tjc", partner_part, my_blocks, preferred_element_type=jnp.float32
    )
    projected = (
        jnp.einsum("tr,jrc->tjc", my_part, my_blocks, preferred_element_type=jnp.float32)
        + lax.ppermute(partner_partial, "seq", perm=pair)
    ).reshape(local_tokens, model_width)
    residual = hidden[0].astype(jnp.float32) + projected
    normed = (
        residual
        * lax.rsqrt(jnp.mean(residual * residual, axis=1, keepdims=True) + 1e-06)
        * norm_gain
    ).astype(jnp.bfloat16)
    logits = jnp.dot(normed, router, preferred_element_type=jnp.float32)
    expert_probs = jax.nn.softmax(logits, axis=1)
    expert_ids = jnp.arange(expert_count, dtype=jnp.int32)
    my_routes = routes[0]
    matches = my_routes[:, :, None] == expert_ids[None, None, :]
    gate_values = jnp.sum(jnp.where(matches, expert_probs[:, None, :], 0.0), axis=2)
    flat_hits = matches.reshape(local_tokens * top_count, expert_count).astype(jnp.int32)
    earlier = jnp.cumsum(flat_hits, axis=0) - flat_hits
    slot_index = jnp.sum(earlier * flat_hits, axis=1).reshape(local_tokens, top_count)
    cell_index = my_routes * capacity + slot_index
    cell_ids = jnp.arange(expert_count * capacity, dtype=jnp.int32)
    placing = jnp.sum(
        (cell_ids[:, None, None] == cell_index[None, :, :]).astype(jnp.int32), axis=2
    ).astype(jnp.bfloat16)
    outgoing = jnp.dot(placing, normed, preferred_element_type=jnp.float32).astype(jnp.bfloat16)
    outgoing = outgoing.reshape(expert_count, capacity, model_width)
    incoming = lax.all_to_all(outgoing, "expert", split_axis=0, concat_axis=0, tiled=True)
    in_width = expert_in.shape[2]
    full_both = lax.all_gather(
        jnp.concatenate([expert_in, expert_out], axis=2), "seq", axis=1, tiled=True
    )
    full_in, full_out = full_both[:, :, :in_width], full_both[:, :, in_width:]
    all_rows = incoming.reshape(-1, model_width)
    gate_up = jnp.dot(all_rows, full_in[0], preferred_element_type=jnp.float32)
    hidden_units = gate_up.shape[1] // 2
    active = (jax.nn.silu(gate_up[:, :hidden_units]) * gate_up[:, hidden_units:]).astype(
        jnp.bfloat16
    )
    produced = lax.dot_general(
        active, full_out[0], (((1,), (1,)), ((), ())), preferred_element_type=jnp.float32
    ).astype(jnp.bfloat16)
    returned = lax.all_to_all(
        produced.reshape(-1, capacity, model_width),
        "expert",
        split_axis=0,
        concat_axis=0,
        tiled=True,
    )
    returned_rows = returned.reshape(-1, model_width)
    combining = jnp.sum(
        jnp.where(cell_index[:, :, None] == cell_ids[None, None, :], gate_values[:, :, None], 0.0),
        axis=1,
    )
    routed_sum = jnp.dot(
        combining,
        returned_rows.astype(jnp.float32),
        precision=lax.Precision.HIGHEST,
        preferred_element_type=jnp.float32,
    )
    layer_out = (residual + routed_sum).astype(jnp.bfloat16)
    return layer_out[None]


def solution(mesh):
    in_specs = (
        P("expert", "seq", None),
        P("expert", "seq", None),
        P("expert", "seq", None),
        P(None, "seq", None),
        P("expert", None),
        P("expert", None),
        P(),
        P(None, "expert"),
        P(),
        P(),
        P("expert", "seq", None),
        P("expert", "seq", None),
        P("expert", "seq", None),
    )
    out_specs = P("expert", "seq", None)
    return jax.shard_map(functools.partial(local, seq_count=mesh.shape["seq"]), mesh=mesh, in_specs=in_specs, out_specs=out_specs, check_vma=False)
```

```python
import functools

import jax
import jax.numpy as jnp
from jax import lax
from jax.experimental import pallas as pl
from jax.sharding import PartitionSpec as P

qk_scale = 192.0 ** (-0.5)
big_negative = -1e30


def request_of(positions, request_ends):
    return jnp.sum((positions[:, None] >= request_ends[None, :]).astype(jnp.int32), axis=1)


def merge_scores(running, scores, allowed, values):
    running_max, running_sum, running_acc = running
    new_max = jnp.maximum(running_max, jnp.max(jnp.where(allowed, scores, big_negative), axis=2))
    weights = jnp.where(allowed, jnp.exp(scores - new_max[:, :, None]), 0.0)
    new_sum = jnp.sum(weights, axis=2)
    new_acc = jnp.einsum(
        "thn,nl->thl", weights.astype(jnp.bfloat16), values, preferred_element_type=jnp.float32
    )
    return (new_max, new_sum, new_acc)


def attention_kernel(q_ref, k_ref, m_ref, o_ref, *, heads, latent_width):
    keys = k_ref[...]
    scores = (
        lax.dot_general(
            q_ref[...], keys, (((1,), (1,)), ((), ())), preferred_element_type=jnp.float32
        )
        * qk_scale
    )
    rows, count = scores.shape
    scores = scores.reshape(rows // heads, heads, count)
    allowed = m_ref[...][:, None, :] > 0.5
    top = jnp.max(jnp.where(allowed, scores, big_negative), axis=2, keepdims=True)
    weights = jnp.where(allowed, jnp.exp(scores - top), 0.0)
    total = jnp.sum(weights, axis=2, keepdims=True)
    acc = jnp.dot(
        weights.reshape(rows, count).astype(jnp.bfloat16),
        keys[:, :latent_width],
        preferred_element_type=jnp.float32,
    )
    o_ref[...] = (
        (acc.reshape(rows // heads, heads, latent_width) / total)
        .reshape(rows, latent_width)
        .astype(o_ref.dtype)
    )


def attend(query_rows, every_key, allowed, heads, latent_width):
    rows, key_width = query_rows.shape
    count = every_key.shape[0]
    flops = 2 * rows * count * (key_width + latent_width)
    return pl.pallas_call(
        functools.partial(attention_kernel, heads=heads, latent_width=latent_width),
        out_shape=jax.ShapeDtypeStruct((rows, latent_width), jnp.bfloat16),
        cost_estimate=pl.CostEstimate(
            flops=flops,
            transcendentals=rows * count,
            bytes_accessed=2 * (rows * key_width + count * key_width + rows * latent_width)
            + 4 * allowed.size,
        ),
    )(query_rows, every_key, allowed)


def expert_kernel(x_ref, w_ref, o_ref, *, in_width):
    weights = w_ref[...]
    gate_up = jnp.dot(x_ref[...], weights[:, :in_width], preferred_element_type=jnp.float32)
    hidden_units = in_width // 2
    gate = gate_up[:, :hidden_units]
    active = (gate / (1.0 + jnp.exp(-gate)) * gate_up[:, hidden_units:]).astype(jnp.bfloat16)
    o_ref[...] = lax.dot_general(
        active, weights[:, in_width:], (((1,), (1,)), ((), ())), preferred_element_type=jnp.float32
    ).astype(o_ref.dtype)


def expert_ffn(rows, both, in_width):
    count, model_width = rows.shape
    hidden_units = in_width // 2
    return pl.pallas_call(
        functools.partial(expert_kernel, in_width=in_width),
        out_shape=jax.ShapeDtypeStruct((count, both.shape[0]), jnp.bfloat16),
        cost_estimate=pl.CostEstimate(
            flops=2 * count * model_width * (in_width + hidden_units),
            transcendentals=count * hidden_units,
            bytes_accessed=2 * (2 * count * model_width + both.size),
        ),
    )(rows, both)


def local(
    hidden,
    queries,
    suffix_latent,
    prefix_latent,
    lengths,
    prefix_of,
    value_up,
    out_proj,
    norm_gain,
    router,
    routes,
    expert_in,
    expert_out,
    seq_count=1,
):
    local_tokens = hidden.shape[1]
    model_width = hidden.shape[2]
    key_width = suffix_latent.shape[2]
    head_count = value_up.shape[0]
    latent_width = value_up.shape[1]
    expert_count = router.shape[1]
    top_count = routes.shape[2]
    capacity = 4 * local_tokens * top_count // (3 * expert_count)
    request_count = lengths.shape[1]
    request_ends = jnp.cumsum(lengths[0])
    my_positions = lax.axis_index("seq") * local_tokens + jnp.arange(local_tokens, dtype=jnp.int32)
    my_requests = request_of(my_positions, request_ends)
    request_ids = jnp.arange(request_count, dtype=jnp.int32)
    chosen = jnp.sum(
        jnp.where(my_requests[:, None] == request_ids[None, :], prefix_of[0][None, :], 0), axis=1
    )
    prefix_pick = chosen[:, None] == jnp.arange(2, dtype=jnp.int32)[None, :]
    query_rows = queries[0].reshape(local_tokens, head_count, key_width)
    key_stack = jnp.concatenate([suffix_latent, prefix_latent], axis=0)
    key_stack = lax.all_gather(key_stack, "seq", axis=1, tiled=True)
    block_count, piece_rows = key_stack.shape[0], key_stack.shape[1]
    key_positions = jnp.arange(piece_rows, dtype=jnp.int32)
    key_requests = request_of(key_positions, request_ends)
    suffix_allowed = (key_requests[None, :] == my_requests[:, None]) & (
        key_positions[None, :] <= my_positions[:, None]
    )
    prefix_allowed = jnp.broadcast_to(
        prefix_pick[:, :, None], (local_tokens, block_count - 1, piece_rows)
    )
    allowed = jnp.concatenate([suffix_allowed[:, None, :], prefix_allowed], axis=1)
    allowed = allowed.reshape(local_tokens, block_count * piece_rows).astype(jnp.float32)
    every_key = key_stack.reshape(block_count * piece_rows, key_width)
    latent_out = attend(
        query_rows.reshape(local_tokens * head_count, key_width),
        every_key,
        allowed,
        head_count,
        latent_width,
    ).reshape(local_tokens, head_count, latent_width)
    value_out = jnp.einsum(
        "thl,hlv->thv", latent_out, value_up, preferred_element_type=jnp.float32
    ).astype(jnp.bfloat16)
    value_out = value_out.reshape(local_tokens, head_count * value_up.shape[2])
    expert_devices = model_width // out_proj.shape[1]
    half_rows = out_proj.shape[0] // 2
    core = lax.axis_index("seq") % 2
    my_rows = lax.dynamic_slice_in_dim(out_proj, core * half_rows, half_rows, axis=0)
    my_blocks = lax.all_to_all(
        jnp.broadcast_to(my_rows[None], (expert_devices,) + my_rows.shape),
        "expert",
        split_axis=0,
        concat_axis=0,
        tiled=True,
    )
    my_blocks, value_out = lax.optimization_barrier((my_blocks, value_out))
    pair = [(i, i ^ 1) for i in range(seq_count)]
    my_part = lax.dynamic_slice_in_dim(value_out, core * half_rows, half_rows, axis=1)
    other_part = lax.dynamic_slice_in_dim(value_out, (1 - core) * half_rows, half_rows, axis=1)
    partner_part = lax.ppermute(other_part, "seq", perm=pair)
    partner_partial = jnp.einsum(
        "tr,jrc->tjc", partner_part, my_blocks, preferred_element_type=jnp.float32
    )
    projected = (
        jnp.einsum("tr,jrc->tjc", my_part, my_blocks, preferred_element_type=jnp.float32)
        + lax.ppermute(partner_partial, "seq", perm=pair)
    ).reshape(local_tokens, model_width)
    residual = hidden[0].astype(jnp.float32) + projected
    normed = (
        residual
        * lax.rsqrt(jnp.mean(residual * residual, axis=1, keepdims=True) + 1e-06)
        * norm_gain
    ).astype(jnp.bfloat16)
    logits = jnp.dot(normed, router, preferred_element_type=jnp.float32)
    expert_probs = jax.nn.softmax(logits, axis=1)
    expert_ids = jnp.arange(expert_count, dtype=jnp.int32)
    my_routes = routes[0]
    matches = my_routes[:, :, None] == expert_ids[None, None, :]
    gate_values = jnp.sum(jnp.where(matches, expert_probs[:, None, :], 0.0), axis=2)
    flat_hits = matches.reshape(local_tokens * top_count, expert_count).astype(jnp.int32)
    earlier = jnp.cumsum(flat_hits, axis=0) - flat_hits
    slot_index = jnp.sum(earlier * flat_hits, axis=1).reshape(local_tokens, top_count)
    cell_index = my_routes * capacity + slot_index
    cell_ids = jnp.arange(expert_count * capacity, dtype=jnp.int32)
    placing = jnp.sum(
        (cell_ids[:, None, None] == cell_index[None, :, :]).astype(jnp.int32), axis=2
    ).astype(jnp.bfloat16)
    outgoing = jnp.dot(placing, normed, preferred_element_type=jnp.float32).astype(jnp.bfloat16)
    outgoing = outgoing.reshape(expert_count, capacity, model_width)
    incoming = lax.all_to_all(outgoing, "expert", split_axis=0, concat_axis=0, tiled=True)
    in_width = expert_in.shape[2]
    full_both = lax.all_gather(
        jnp.concatenate([expert_in, expert_out], axis=2), "seq", axis=1, tiled=True
    )
    all_rows = incoming.reshape(-1, model_width)
    produced = expert_ffn(all_rows, full_both[0], in_width)
    returned = lax.all_to_all(
        produced.reshape(-1, capacity, model_width),
        "expert",
        split_axis=0,
        concat_axis=0,
        tiled=True,
    )
    returned_rows = returned.reshape(-1, model_width)
    combining = jnp.sum(
        jnp.where(cell_index[:, :, None] == cell_ids[None, None, :], gate_values[:, :, None], 0.0),
        axis=1,
    )
    routed_sum = jnp.dot(
        combining,
        returned_rows.astype(jnp.float32),
        precision=lax.Precision.HIGHEST,
        preferred_element_type=jnp.float32,
    )
    layer_out = (residual + routed_sum).astype(jnp.bfloat16)
    return layer_out[None]


def solution(mesh):
    in_specs = (
        P("expert", "seq", None),
        P("expert", "seq", None),
        P("expert", "seq", None),
        P(None, "seq", None),
        P("expert", None),
        P("expert", None),
        P(),
        P(None, "expert"),
        P(),
        P(),
        P("expert", "seq", None),
        P("expert", "seq", None),
        P("expert", "seq", None),
    )
    out_specs = P("expert", "seq", None)
    return jax.shard_map(functools.partial(local, seq_count=mesh.shape["seq"]), mesh=mesh, in_specs=in_specs, out_specs=out_specs, check_vma=False)
```

```python
import functools

import jax
import jax.numpy as jnp
from jax import lax
from jax.experimental import pallas as pl
from jax.sharding import PartitionSpec as P

qk_scale = 192.0 ** (-0.5)
big_negative = -1e30


def request_of(positions, request_ends):
    return jnp.sum((positions[:, None] >= request_ends[None, :]).astype(jnp.int32), axis=1)


def merge_scores(running, scores, allowed, values):
    running_max, running_sum, running_acc = running
    new_max = jnp.maximum(running_max, jnp.max(jnp.where(allowed, scores, big_negative), axis=2))
    weights = jnp.where(allowed, jnp.exp(scores - new_max[:, :, None]), 0.0)
    new_sum = jnp.sum(weights, axis=2)
    new_acc = jnp.einsum(
        "thn,nl->thl", weights.astype(jnp.bfloat16), values, preferred_element_type=jnp.float32
    )
    return (new_max, new_sum, new_acc)


def attention_kernel(q_ref, k_ref, m_ref, o_ref, *, heads, latent_width):
    keys = k_ref[...]
    scores = (
        lax.dot_general(
            q_ref[...], keys, (((1,), (1,)), ((), ())), preferred_element_type=jnp.float32
        )
        * qk_scale
    )
    rows, count = scores.shape
    scores = scores.reshape(rows // heads, heads, count)
    allowed = m_ref[...][:, None, :] > 0.5
    top = jnp.max(jnp.where(allowed, scores, big_negative), axis=2, keepdims=True)
    weights = jnp.where(allowed, jnp.exp(scores - top), 0.0)
    total = jnp.sum(weights, axis=2, keepdims=True)
    acc = jnp.dot(
        weights.reshape(rows, count).astype(jnp.bfloat16),
        keys[:, :latent_width],
        preferred_element_type=jnp.float32,
    )
    o_ref[...] = (
        (acc.reshape(rows // heads, heads, latent_width) / total)
        .reshape(rows, latent_width)
        .astype(o_ref.dtype)
    )


def attend(query_rows, every_key, allowed, heads, latent_width):
    rows, key_width = query_rows.shape
    count = every_key.shape[0]
    flops = 2 * rows * count * (key_width + latent_width)
    return pl.pallas_call(
        functools.partial(attention_kernel, heads=heads, latent_width=latent_width),
        out_shape=jax.ShapeDtypeStruct((rows, latent_width), jnp.bfloat16),
        cost_estimate=pl.CostEstimate(
            flops=flops,
            transcendentals=rows * count,
            bytes_accessed=2 * (rows * key_width + count * key_width + rows * latent_width)
            + 4 * allowed.size,
        ),
    )(query_rows, every_key, allowed)


def expert_kernel(x_ref, w_ref, o_ref, *, in_width):
    weights = w_ref[...]
    gate_up = jnp.dot(x_ref[...], weights[:, :in_width], preferred_element_type=jnp.float32)
    hidden_units = in_width // 2
    gate = gate_up[:, :hidden_units]
    active = (gate / (1.0 + jnp.exp(-gate)) * gate_up[:, hidden_units:]).astype(jnp.bfloat16)
    o_ref[...] = lax.dot_general(
        active, weights[:, in_width:], (((1,), (1,)), ((), ())), preferred_element_type=jnp.float32
    ).astype(o_ref.dtype)


def expert_ffn(rows, both, in_width):
    count, model_width = rows.shape
    hidden_units = in_width // 2
    return pl.pallas_call(
        functools.partial(expert_kernel, in_width=in_width),
        out_shape=jax.ShapeDtypeStruct((count, both.shape[0]), jnp.bfloat16),
        cost_estimate=pl.CostEstimate(
            flops=2 * count * model_width * (in_width + hidden_units),
            transcendentals=count * hidden_units,
            bytes_accessed=2 * (2 * count * model_width + both.size),
        ),
    )(rows, both)


def local(
    hidden,
    queries,
    suffix_latent,
    prefix_latent,
    lengths,
    prefix_of,
    value_up,
    out_proj,
    norm_gain,
    router,
    routes,
    expert_in,
    expert_out,
    seq_count=1,
):
    local_tokens = hidden.shape[1]
    model_width = hidden.shape[2]
    key_width = suffix_latent.shape[2]
    head_count = value_up.shape[0]
    latent_width = value_up.shape[1]
    expert_count = router.shape[1]
    top_count = routes.shape[2]
    capacity = 4 * local_tokens * top_count // (3 * expert_count)
    request_count = lengths.shape[1]
    request_ends = jnp.cumsum(lengths[0])
    my_positions = lax.axis_index("seq") * local_tokens + jnp.arange(local_tokens, dtype=jnp.int32)
    my_requests = request_of(my_positions, request_ends)
    request_ids = jnp.arange(request_count, dtype=jnp.int32)
    chosen = jnp.sum(
        jnp.where(my_requests[:, None] == request_ids[None, :], prefix_of[0][None, :], 0), axis=1
    )
    prefix_pick = chosen[:, None] == jnp.arange(2, dtype=jnp.int32)[None, :]
    query_rows = queries[0].reshape(local_tokens, head_count, key_width)
    key_stack = jnp.concatenate([suffix_latent, prefix_latent], axis=0)
    key_stack = lax.all_gather(key_stack, "seq", axis=1, tiled=True)
    block_count, piece_rows = key_stack.shape[0], key_stack.shape[1]
    key_positions = jnp.arange(piece_rows, dtype=jnp.int32)
    key_requests = request_of(key_positions, request_ends)
    suffix_allowed = (key_requests[None, :] == my_requests[:, None]) & (
        key_positions[None, :] <= my_positions[:, None]
    )
    prefix_allowed = jnp.broadcast_to(
        prefix_pick[:, :, None], (local_tokens, block_count - 1, piece_rows)
    )
    allowed = jnp.concatenate([suffix_allowed[:, None, :], prefix_allowed], axis=1)
    allowed = allowed.reshape(local_tokens, block_count * piece_rows).astype(jnp.float32)
    every_key = key_stack.reshape(block_count * piece_rows, key_width)
    expert_devices = model_width // out_proj.shape[1]
    half_rows = out_proj.shape[0] // 2
    core = lax.axis_index("seq") % 2
    my_rows = lax.dynamic_slice_in_dim(out_proj, core * half_rows, half_rows, axis=0)
    my_blocks = lax.all_to_all(
        jnp.broadcast_to(my_rows[None], (expert_devices,) + my_rows.shape),
        "expert",
        split_axis=0,
        concat_axis=0,
        tiled=True,
    )
    my_blocks, every_key = lax.optimization_barrier((my_blocks, every_key))
    latent_out = attend(
        query_rows.reshape(local_tokens * head_count, key_width),
        every_key,
        allowed,
        head_count,
        latent_width,
    ).reshape(local_tokens, head_count, latent_width)
    value_out = jnp.einsum(
        "thl,hlv->thv", latent_out, value_up, preferred_element_type=jnp.float32
    ).astype(jnp.bfloat16)
    value_out = value_out.reshape(local_tokens, head_count * value_up.shape[2])
    pair = [(i, i ^ 1) for i in range(seq_count)]
    other_blocks = lax.ppermute(my_blocks, "seq", perm=pair)
    my_part = lax.dynamic_slice_in_dim(value_out, core * half_rows, half_rows, axis=1)
    other_part = lax.dynamic_slice_in_dim(value_out, (1 - core) * half_rows, half_rows, axis=1)
    projected = (
        jnp.einsum("tr,jrc->tjc", my_part, my_blocks, preferred_element_type=jnp.float32)
        + jnp.einsum("tr,jrc->tjc", other_part, other_blocks, preferred_element_type=jnp.float32)
    ).reshape(local_tokens, model_width)
    residual = hidden[0].astype(jnp.float32) + projected
    normed = (
        residual
        * lax.rsqrt(jnp.mean(residual * residual, axis=1, keepdims=True) + 1e-06)
        * norm_gain
    ).astype(jnp.bfloat16)
    logits = jnp.dot(normed, router, preferred_element_type=jnp.float32)
    expert_probs = jax.nn.softmax(logits, axis=1)
    expert_ids = jnp.arange(expert_count, dtype=jnp.int32)
    my_routes = routes[0]
    matches = my_routes[:, :, None] == expert_ids[None, None, :]
    gate_values = jnp.sum(jnp.where(matches, expert_probs[:, None, :], 0.0), axis=2)
    flat_hits = matches.reshape(local_tokens * top_count, expert_count).astype(jnp.int32)
    earlier = jnp.cumsum(flat_hits, axis=0) - flat_hits
    slot_index = jnp.sum(earlier * flat_hits, axis=1).reshape(local_tokens, top_count)
    cell_index = my_routes * capacity + slot_index
    cell_ids = jnp.arange(expert_count * capacity, dtype=jnp.int32)
    placing = jnp.sum(
        (cell_ids[:, None, None] == cell_index[None, :, :]).astype(jnp.int32), axis=2
    ).astype(jnp.bfloat16)
    outgoing = jnp.dot(placing, normed, preferred_element_type=jnp.float32).astype(jnp.bfloat16)
    outgoing = outgoing.reshape(expert_count, capacity, model_width)
    incoming = lax.all_to_all(outgoing, "expert", split_axis=0, concat_axis=0, tiled=True)
    in_width = expert_in.shape[2]
    full_both = lax.all_gather(
        jnp.concatenate([expert_in, expert_out], axis=2), "seq", axis=1, tiled=True
    )
    all_rows = incoming.reshape(-1, model_width)
    produced = expert_ffn(all_rows, full_both[0], in_width)
    returned = lax.all_to_all(
        produced.reshape(-1, capacity, model_width),
        "expert",
        split_axis=0,
        concat_axis=0,
        tiled=True,
    )
    returned_rows = returned.reshape(-1, model_width)
    combining = jnp.sum(
        jnp.where(cell_index[:, :, None] == cell_ids[None, None, :], gate_values[:, :, None], 0.0),
        axis=1,
    )
    routed_sum = jnp.dot(
        combining,
        returned_rows.astype(jnp.float32),
        precision=lax.Precision.HIGHEST,
        preferred_element_type=jnp.float32,
    )
    layer_out = (residual + routed_sum).astype(jnp.bfloat16)
    return layer_out[None]


def solution(mesh):
    in_specs = (
        P("expert", "seq", None),
        P("expert", "seq", None),
        P("expert", "seq", None),
        P(None, "seq", None),
        P("expert", None),
        P("expert", None),
        P(),
        P(None, "expert"),
        P(),
        P(),
        P("expert", "seq", None),
        P("expert", "seq", None),
        P("expert", "seq", None),
    )
    out_specs = P("expert", "seq", None)
    return jax.shard_map(functools.partial(local, seq_count=mesh.shape["seq"]), mesh=mesh, in_specs=in_specs, out_specs=out_specs, check_vma=False)
```

```python
import functools

import jax
import jax.numpy as jnp
from jax import lax
from jax.experimental import pallas as pl
from jax.sharding import PartitionSpec as P

qk_scale = 192.0 ** (-0.5)
big_negative = -1e30


def request_of(positions, request_ends):
    return jnp.sum((positions[:, None] >= request_ends[None, :]).astype(jnp.int32), axis=1)


def merge_scores(running, scores, allowed, values):
    running_max, running_sum, running_acc = running
    new_max = jnp.maximum(running_max, jnp.max(jnp.where(allowed, scores, big_negative), axis=2))
    weights = jnp.where(allowed, jnp.exp(scores - new_max[:, :, None]), 0.0)
    new_sum = jnp.sum(weights, axis=2)
    new_acc = jnp.einsum(
        "thn,nl->thl", weights.astype(jnp.bfloat16), values, preferred_element_type=jnp.float32
    )
    return (new_max, new_sum, new_acc)


def attention_kernel(q_ref, k_ref, m_ref, o_ref, *, heads, latent_width):
    keys = k_ref[...]
    scores = (
        lax.dot_general(
            q_ref[...], keys, (((1,), (1,)), ((), ())), preferred_element_type=jnp.float32
        )
        * qk_scale
    )
    rows, count = scores.shape
    scores = scores.reshape(rows // heads, heads, count)
    allowed = m_ref[...][:, None, :] > 0.5
    top = jnp.max(jnp.where(allowed, scores, big_negative), axis=2, keepdims=True)
    weights = jnp.where(allowed, jnp.exp(scores - top), 0.0)
    total = jnp.sum(weights, axis=2, keepdims=True)
    acc = jnp.dot(
        weights.reshape(rows, count).astype(jnp.bfloat16),
        keys[:, :latent_width],
        preferred_element_type=jnp.float32,
    )
    o_ref[...] = (
        (acc.reshape(rows // heads, heads, latent_width) / total)
        .reshape(rows, latent_width)
        .astype(o_ref.dtype)
    )


def attend(query_rows, every_key, allowed, heads, latent_width):
    rows, key_width = query_rows.shape
    count = every_key.shape[0]
    flops = 2 * rows * count * (key_width + latent_width)
    return pl.pallas_call(
        functools.partial(attention_kernel, heads=heads, latent_width=latent_width),
        out_shape=jax.ShapeDtypeStruct((rows, latent_width), jnp.bfloat16),
        cost_estimate=pl.CostEstimate(
            flops=flops,
            transcendentals=rows * count,
            bytes_accessed=2 * (rows * key_width + count * key_width + rows * latent_width)
            + 4 * allowed.size,
        ),
    )(query_rows, every_key, allowed)


def expert_kernel(x_ref, w_ref, o_ref, *, in_width):
    weights = w_ref[...]
    gate_up = jnp.dot(x_ref[...], weights[:, :in_width], preferred_element_type=jnp.float32)
    hidden_units = in_width // 2
    gate = gate_up[:, :hidden_units]
    active = (gate / (1.0 + jnp.exp(-gate)) * gate_up[:, hidden_units:]).astype(jnp.bfloat16)
    o_ref[...] = lax.dot_general(
        active, weights[:, in_width:], (((1,), (1,)), ((), ())), preferred_element_type=jnp.float32
    ).astype(o_ref.dtype)


def expert_ffn(rows, both, in_width):
    count, model_width = rows.shape
    hidden_units = in_width // 2
    return pl.pallas_call(
        functools.partial(expert_kernel, in_width=in_width),
        out_shape=jax.ShapeDtypeStruct((count, both.shape[0]), jnp.bfloat16),
        cost_estimate=pl.CostEstimate(
            flops=2 * count * model_width * (in_width + hidden_units),
            transcendentals=count * hidden_units,
            bytes_accessed=2 * (2 * count * model_width + both.size),
        ),
    )(rows, both)


def local(
    hidden,
    queries,
    suffix_latent,
    prefix_latent,
    lengths,
    prefix_of,
    value_up,
    out_proj,
    norm_gain,
    router,
    routes,
    expert_in,
    expert_out,
    seq_count=1,
):
    local_tokens = hidden.shape[1]
    model_width = hidden.shape[2]
    key_width = suffix_latent.shape[2]
    head_count = value_up.shape[0]
    latent_width = value_up.shape[1]
    expert_count = router.shape[1]
    top_count = routes.shape[2]
    capacity = 4 * local_tokens * top_count // (3 * expert_count)
    request_count = lengths.shape[1]
    request_ends = jnp.cumsum(lengths[0])
    my_positions = lax.axis_index("seq") * local_tokens + jnp.arange(local_tokens, dtype=jnp.int32)
    my_requests = request_of(my_positions, request_ends)
    request_ids = jnp.arange(request_count, dtype=jnp.int32)
    chosen = jnp.sum(
        jnp.where(my_requests[:, None] == request_ids[None, :], prefix_of[0][None, :], 0), axis=1
    )
    prefix_pick = chosen[:, None] == jnp.arange(2, dtype=jnp.int32)[None, :]
    query_rows = queries[0].reshape(local_tokens, head_count, key_width)
    key_stack = jnp.concatenate([suffix_latent, prefix_latent], axis=0)
    key_stack = lax.all_gather(key_stack, "seq", axis=1, tiled=True)
    block_count, piece_rows = key_stack.shape[0], key_stack.shape[1]
    key_positions = jnp.arange(piece_rows, dtype=jnp.int32)
    key_requests = request_of(key_positions, request_ends)
    suffix_allowed = (key_requests[None, :] == my_requests[:, None]) & (
        key_positions[None, :] <= my_positions[:, None]
    )
    prefix_allowed = jnp.broadcast_to(
        prefix_pick[:, :, None], (local_tokens, block_count - 1, piece_rows)
    )
    allowed = jnp.concatenate([suffix_allowed[:, None, :], prefix_allowed], axis=1)
    allowed = allowed.reshape(local_tokens, block_count * piece_rows).astype(jnp.float32)
    every_key = key_stack.reshape(block_count * piece_rows, key_width)
    latent_out = attend(
        query_rows.reshape(local_tokens * head_count, key_width),
        every_key,
        allowed,
        head_count,
        latent_width,
    ).reshape(local_tokens, head_count, latent_width)
    value_out = jnp.einsum(
        "thl,hlv->thv", latent_out, value_up, preferred_element_type=jnp.float32
    ).astype(jnp.bfloat16)
    value_out = value_out.reshape(local_tokens, head_count * value_up.shape[2])
    expert_devices = model_width // out_proj.shape[1]
    half_rows = out_proj.shape[0] // 2
    core = lax.axis_index("seq") % 2
    my_rows = lax.dynamic_slice_in_dim(out_proj, core * half_rows, half_rows, axis=0)
    my_blocks = lax.all_to_all(
        jnp.broadcast_to(my_rows[None], (expert_devices,) + my_rows.shape),
        "expert",
        split_axis=0,
        concat_axis=0,
        tiled=True,
    )
    my_blocks, value_out = lax.optimization_barrier((my_blocks, value_out))
    my_blocks, expert_in, expert_out = lax.optimization_barrier((my_blocks, expert_in, expert_out))
    pair = [(i, i ^ 1) for i in range(seq_count)]
    my_part = lax.dynamic_slice_in_dim(value_out, core * half_rows, half_rows, axis=1)
    other_part = lax.dynamic_slice_in_dim(value_out, (1 - core) * half_rows, half_rows, axis=1)
    partner_part = lax.ppermute(other_part, "seq", perm=pair)
    partner_partial = jnp.einsum(
        "tr,jrc->tjc", partner_part, my_blocks, preferred_element_type=jnp.float32
    )
    projected = (
        jnp.einsum("tr,jrc->tjc", my_part, my_blocks, preferred_element_type=jnp.float32)
        + lax.ppermute(partner_partial, "seq", perm=pair)
    ).reshape(local_tokens, model_width)
    residual = hidden[0].astype(jnp.float32) + projected
    normed = (
        residual
        * lax.rsqrt(jnp.mean(residual * residual, axis=1, keepdims=True) + 1e-06)
        * norm_gain
    ).astype(jnp.bfloat16)
    logits = jnp.dot(normed, router, preferred_element_type=jnp.float32)
    expert_probs = jax.nn.softmax(logits, axis=1)
    expert_ids = jnp.arange(expert_count, dtype=jnp.int32)
    my_routes = routes[0]
    matches = my_routes[:, :, None] == expert_ids[None, None, :]
    gate_values = jnp.sum(jnp.where(matches, expert_probs[:, None, :], 0.0), axis=2)
    flat_hits = matches.reshape(local_tokens * top_count, expert_count).astype(jnp.int32)
    earlier = jnp.cumsum(flat_hits, axis=0) - flat_hits
    slot_index = jnp.sum(earlier * flat_hits, axis=1).reshape(local_tokens, top_count)
    cell_index = my_routes * capacity + slot_index
    cell_ids = jnp.arange(expert_count * capacity, dtype=jnp.int32)
    placing = jnp.sum(
        (cell_ids[:, None, None] == cell_index[None, :, :]).astype(jnp.int32), axis=2
    ).astype(jnp.bfloat16)
    outgoing = jnp.dot(placing, normed, preferred_element_type=jnp.float32).astype(jnp.bfloat16)
    outgoing = outgoing.reshape(expert_count, capacity, model_width)
    incoming = lax.all_to_all(outgoing, "expert", split_axis=0, concat_axis=0, tiled=True)
    in_width = expert_in.shape[2]
    full_both = lax.all_gather(
        jnp.concatenate([expert_in, expert_out], axis=2), "seq", axis=1, tiled=True
    )
    all_rows = incoming.reshape(-1, model_width)
    produced = expert_ffn(all_rows, full_both[0], in_width)
    returned = lax.all_to_all(
        produced.reshape(-1, capacity, model_width),
        "expert",
        split_axis=0,
        concat_axis=0,
        tiled=True,
    )
    returned_rows = returned.reshape(-1, model_width)
    combining = jnp.sum(
        jnp.where(cell_index[:, :, None] == cell_ids[None, None, :], gate_values[:, :, None], 0.0),
        axis=1,
    )
    routed_sum = jnp.dot(
        combining,
        returned_rows.astype(jnp.float32),
        precision=lax.Precision.HIGHEST,
        preferred_element_type=jnp.float32,
    )
    layer_out = (residual + routed_sum).astype(jnp.bfloat16)
    return layer_out[None]


def solution(mesh):
    in_specs = (
        P("expert", "seq", None),
        P("expert", "seq", None),
        P("expert", "seq", None),
        P(None, "seq", None),
        P("expert", None),
        P("expert", None),
        P(),
        P(None, "expert"),
        P(),
        P(),
        P("expert", "seq", None),
        P("expert", "seq", None),
        P("expert", "seq", None),
    )
    out_specs = P("expert", "seq", None)
    return jax.shard_map(functools.partial(local, seq_count=mesh.shape["seq"]), mesh=mesh, in_specs=in_specs, out_specs=out_specs, check_vma=False)
```

```python
import functools

import jax
import jax.numpy as jnp
from jax import lax
from jax.experimental import pallas as pl
from jax.sharding import PartitionSpec as P

qk_scale = 192.0 ** (-0.5)
big_negative = -1e30


def request_of(positions, request_ends):
    return jnp.sum((positions[:, None] >= request_ends[None, :]).astype(jnp.int32), axis=1)


def merge_scores(running, scores, allowed, values):
    running_max, running_sum, running_acc = running
    new_max = jnp.maximum(running_max, jnp.max(jnp.where(allowed, scores, big_negative), axis=2))
    weights = jnp.where(allowed, jnp.exp(scores - new_max[:, :, None]), 0.0)
    new_sum = jnp.sum(weights, axis=2)
    new_acc = jnp.einsum(
        "thn,nl->thl", weights.astype(jnp.bfloat16), values, preferred_element_type=jnp.float32
    )
    return (new_max, new_sum, new_acc)


def attention_kernel(q_ref, k_ref, m_ref, o_ref, *, heads, latent_width):
    keys = k_ref[...]
    scores = (
        lax.dot_general(
            q_ref[...], keys, (((1,), (1,)), ((), ())), preferred_element_type=jnp.float32
        )
        * qk_scale
    )
    rows, count = scores.shape
    scores = scores.reshape(rows // heads, heads, count)
    allowed = m_ref[...][:, None, :] > 0.5
    top = jnp.max(jnp.where(allowed, scores, big_negative), axis=2, keepdims=True)
    weights = jnp.where(allowed, jnp.exp(scores - top), 0.0)
    total = jnp.sum(weights, axis=2, keepdims=True)
    acc = jnp.dot(
        weights.reshape(rows, count).astype(jnp.bfloat16),
        keys[:, :latent_width],
        preferred_element_type=jnp.float32,
    )
    o_ref[...] = (
        (acc.reshape(rows // heads, heads, latent_width) / total)
        .reshape(rows, latent_width)
        .astype(o_ref.dtype)
    )


def attend(query_rows, every_key, allowed, heads, latent_width):
    rows, key_width = query_rows.shape
    count = every_key.shape[0]
    flops = 2 * rows * count * (key_width + latent_width)
    return pl.pallas_call(
        functools.partial(attention_kernel, heads=heads, latent_width=latent_width),
        out_shape=jax.ShapeDtypeStruct((rows, latent_width), jnp.bfloat16),
        cost_estimate=pl.CostEstimate(
            flops=flops,
            transcendentals=rows * count,
            bytes_accessed=2 * (rows * key_width + count * key_width + rows * latent_width)
            + 4 * allowed.size,
        ),
    )(query_rows, every_key, allowed)


def expert_kernel(x_ref, w_ref, o_ref, *, in_width):
    weights = w_ref[...]
    gate_up = jnp.dot(x_ref[...], weights[:, :in_width], preferred_element_type=jnp.float32)
    hidden_units = in_width // 2
    gate = gate_up[:, :hidden_units]
    active = (gate / (1.0 + jnp.exp(-gate)) * gate_up[:, hidden_units:]).astype(jnp.bfloat16)
    o_ref[...] = lax.dot_general(
        active, weights[:, in_width:], (((1,), (1,)), ((), ())), preferred_element_type=jnp.float32
    ).astype(o_ref.dtype)


def expert_ffn(rows, both, in_width):
    count, model_width = rows.shape
    hidden_units = in_width // 2
    return pl.pallas_call(
        functools.partial(expert_kernel, in_width=in_width),
        out_shape=jax.ShapeDtypeStruct((count, both.shape[0]), jnp.bfloat16),
        cost_estimate=pl.CostEstimate(
            flops=2 * count * model_width * (in_width + hidden_units),
            transcendentals=count * hidden_units,
            bytes_accessed=2 * (2 * count * model_width + both.size),
        ),
    )(rows, both)


def local(
    hidden,
    queries,
    suffix_latent,
    prefix_latent,
    lengths,
    prefix_of,
    value_up,
    out_proj,
    norm_gain,
    router,
    routes,
    expert_in,
    expert_out,
    seq_count=1,
):
    local_tokens = hidden.shape[1]
    model_width = hidden.shape[2]
    key_width = suffix_latent.shape[2]
    head_count = value_up.shape[0]
    latent_width = value_up.shape[1]
    expert_count = router.shape[1]
    top_count = routes.shape[2]
    capacity = 4 * local_tokens * top_count // (3 * expert_count)
    request_count = lengths.shape[1]
    request_ends = jnp.cumsum(lengths[0])
    my_positions = lax.axis_index("seq") * local_tokens + jnp.arange(local_tokens, dtype=jnp.int32)
    my_requests = request_of(my_positions, request_ends)
    request_ids = jnp.arange(request_count, dtype=jnp.int32)
    chosen = jnp.sum(
        jnp.where(my_requests[:, None] == request_ids[None, :], prefix_of[0][None, :], 0), axis=1
    )
    prefix_pick = chosen[:, None] == jnp.arange(2, dtype=jnp.int32)[None, :]
    query_rows = queries[0].reshape(local_tokens, head_count, key_width)
    key_stack = jnp.concatenate([suffix_latent, prefix_latent], axis=0)
    key_stack = lax.all_gather(key_stack, "seq", axis=1, tiled=True)
    block_count, piece_rows = key_stack.shape[0], key_stack.shape[1]
    key_positions = jnp.arange(piece_rows, dtype=jnp.int32)
    key_requests = request_of(key_positions, request_ends)
    suffix_allowed = (key_requests[None, :] == my_requests[:, None]) & (
        key_positions[None, :] <= my_positions[:, None]
    )
    prefix_allowed = jnp.broadcast_to(
        prefix_pick[:, :, None], (local_tokens, block_count - 1, piece_rows)
    )
    allowed = jnp.concatenate([suffix_allowed[:, None, :], prefix_allowed], axis=1)
    allowed = allowed.reshape(local_tokens, block_count * piece_rows).astype(jnp.float32)
    every_key = key_stack.reshape(block_count * piece_rows, key_width)
    latent_out = attend(
        query_rows.reshape(local_tokens * head_count, key_width),
        every_key,
        allowed,
        head_count,
        latent_width,
    ).reshape(local_tokens, head_count, latent_width)
    value_out = jnp.einsum(
        "thl,hlv->thv", latent_out, value_up, preferred_element_type=jnp.float32
    ).astype(jnp.bfloat16)
    value_out = value_out.reshape(local_tokens, head_count * value_up.shape[2])
    expert_devices = model_width // out_proj.shape[1]
    half_rows = out_proj.shape[0] // 2
    core = lax.axis_index("seq") % 2
    my_rows = lax.dynamic_slice_in_dim(out_proj, core * half_rows, half_rows, axis=0)
    my_blocks = lax.all_to_all(
        jnp.broadcast_to(my_rows[None], (expert_devices,) + my_rows.shape),
        "expert",
        split_axis=0,
        concat_axis=0,
        tiled=True,
    )
    my_blocks, value_out = lax.optimization_barrier((my_blocks, value_out))
    pair = [(i, i ^ 1) for i in range(seq_count)]
    my_part = lax.dynamic_slice_in_dim(value_out, core * half_rows, half_rows, axis=1)
    other_part = lax.dynamic_slice_in_dim(value_out, (1 - core) * half_rows, half_rows, axis=1)
    partner_part = lax.ppermute(other_part, "seq", perm=pair)
    partner_partial = jnp.einsum(
        "tr,jrc->tjc", partner_part, my_blocks, preferred_element_type=jnp.float32
    )
    projected = (
        jnp.einsum("tr,jrc->tjc", my_part, my_blocks, preferred_element_type=jnp.float32)
        + lax.ppermute(partner_partial, "seq", perm=pair)
    ).reshape(local_tokens, model_width)
    residual = hidden[0].astype(jnp.float32) + projected
    normed = (
        residual
        * lax.rsqrt(jnp.mean(residual * residual, axis=1, keepdims=True) + 1e-06)
        * norm_gain
    ).astype(jnp.bfloat16)
    logits = jnp.dot(normed, router, preferred_element_type=jnp.float32)
    expert_probs = jax.nn.softmax(logits, axis=1)
    expert_ids = jnp.arange(expert_count, dtype=jnp.int32)
    my_routes = routes[0]
    matches = my_routes[:, :, None] == expert_ids[None, None, :]
    gate_values = jnp.sum(jnp.where(matches, expert_probs[:, None, :], 0.0), axis=2)
    flat_hits = matches.reshape(local_tokens * top_count, expert_count).astype(jnp.int32)
    earlier = jnp.cumsum(flat_hits, axis=0) - flat_hits
    slot_index = jnp.sum(earlier * flat_hits, axis=1).reshape(local_tokens, top_count)
    cell_index = my_routes * capacity + slot_index
    cell_ids = jnp.arange(expert_count * capacity, dtype=jnp.int32)
    placing = jnp.sum(
        (cell_ids[:, None, None] == cell_index[None, :, :]).astype(jnp.int32), axis=2
    ).astype(jnp.bfloat16)
    outgoing = jnp.dot(placing, normed, preferred_element_type=jnp.float32).astype(jnp.bfloat16)
    outgoing = outgoing.reshape(expert_count, capacity, model_width)
    incoming = lax.all_to_all(outgoing, "expert", split_axis=0, concat_axis=0, tiled=True)
    in_width = expert_in.shape[2]
    full_both = lax.all_gather(
        jnp.concatenate([expert_in, expert_out], axis=2), "seq", axis=1, tiled=True
    )
    all_rows = incoming.reshape(-1, model_width)
    produced = expert_ffn(all_rows, full_both[0], in_width)
    returned = lax.all_to_all(
        produced.reshape(-1, capacity, model_width),
        "expert",
        split_axis=0,
        concat_axis=0,
        tiled=True,
    )
    returned_rows = returned.reshape(-1, model_width)
    combining = jnp.sum(
        jnp.where(cell_index[:, :, None] == cell_ids[None, None, :], gate_values[:, :, None], 0.0),
        axis=1,
    )
    routed_sum = jnp.zeros((local_tokens, model_width), jnp.float32)
    rest = combining
    for _ in range(3):
        part = rest.astype(jnp.bfloat16)
        rest = rest - part.astype(jnp.float32)
        routed_sum = routed_sum + jnp.dot(
            part, returned_rows, preferred_element_type=jnp.float32
        )
    layer_out = (residual + routed_sum).astype(jnp.bfloat16)
    return layer_out[None]


def solution(mesh):
    in_specs = (
        P("expert", "seq", None),
        P("expert", "seq", None),
        P("expert", "seq", None),
        P(None, "seq", None),
        P("expert", None),
        P("expert", None),
        P(),
        P(None, "expert"),
        P(),
        P(),
        P("expert", "seq", None),
        P("expert", "seq", None),
        P("expert", "seq", None),
    )
    out_specs = P("expert", "seq", None)
    return jax.shard_map(functools.partial(local, seq_count=mesh.shape["seq"]), mesh=mesh, in_specs=in_specs, out_specs=out_specs, check_vma=False)
```
